512 devices in a mesh: section: 8 (over x, core), frames: 4 (over y), space: 16 (over z).
Axes of the slice: x: 4, y: 4, z: 16, core: 2. Of those that a mesh axis runs over, the one named last changes fastest.
Arguments:
- base_frames: bfloat16 [8, 32, 128, 8, 128], P(None, 'frames', 'space'), may hold values from -6 to 6
- section_noise: bfloat16 [8, 8, 32, 128, 8, 128], P('section', None, 'frames', 'space'), may hold values from -6 to 6
- noise_levels: bfloat16 [8], P('section'), may hold values from 0.29882812 to 1
- spatial_kernel: bfloat16 [8, 9, 128, 128], P('section'), may hold values from -0.15625 to 0.15625
- temporal_kernel: bfloat16 [8, 3, 128, 128], P('section'), may hold values from -0.15625 to 0.15625
- output_weight: bfloat16 [8, 128, 128], P('section'), may hold values from -0.5 to 0.5
Outputs:
- denoised: bfloat16 [8, 8, 32, 128, 8, 128], P('section', None, 'frames', 'space')
The draws below stay inside these ranges and needn't reach their ends.
All inputs are finite; a program needn't handle non-finite values.
Results may differ from the reference program's by a relative error of at most 0.008.
Values may be sent and summed in bfloat16 or wider, within the bound.
No kernel may reach another device: no remote copies, remote signals or barrier semaphores. Data moves between devices by JAX's collectives and lax.ppermute only.
A program may use at most 64 MiB of HBM per device.

```python
import math
import jax
import jax.numpy as jnp
from jax import lax

C = 128
VIDEOS = 8
COLS = 8
SECTIONS = 8
FRAMES = 32
ROWS = 128


def steps_of(rng, dims, cuts, low, top_value):
    loudness = 1.0
    for dim, blocks in cuts:
        heights = jax.random.uniform(jax.random.fold_in(jax.random.fold_in(rng, 6), dim), (blocks,), jnp.float32, low / len(cuts), top_value / len(cuts))
        loudness = loudness * jnp.repeat(jnp.exp(heights), dims[dim] // blocks).reshape((-1,) + (1,) * (len(dims) - 1 - dim))
    return loudness


def normal_values(stream_key, extent, width, reach, pieces=(), dtype=jnp.bfloat16):
    drawn = jax.random.normal(stream_key, extent, jnp.float32) * width
    if len(pieces) > 0:
        drawn = steps_of(stream_key, extent, pieces, -0.22, 0.18) * drawn
    return jnp.clip(drawn, min=-reach, max=reach).astype(dtype)


def setup_inputs(seed: int = 0) -> dict:
    splits = jax.random.split(jax.random.key(seed), 7)
    return {
        "base_frames": normal_values(splits[0], (VIDEOS, FRAMES, ROWS, COLS, C), 1.0, 6.0, ((1, 4), (2, 16))),
        "section_noise": normal_values(splits[1], (SECTIONS, VIDEOS, FRAMES, ROWS, COLS, C), 1.0, 6.0, ((0, 8), (2, 4), (3, 16))),
        "noise_levels": jnp.clip(jnp.exp(math.log(1.0) - 1.2078867 * jax.random.uniform(splits[2], (SECTIONS,), jnp.float32) ** steps_of(splits[2], (SECTIONS,), ((0, 8),), -0.2, 0.2)), 0.29882812, 1.0).astype(jnp.bfloat16),
        "spatial_kernel": normal_values(splits[3], (SECTIONS, 9, C, C), (12 * C) ** -0.5, 0.15625, ((0, 8),)),
        "temporal_kernel": normal_values(splits[4], (SECTIONS, 3, C, C), (12 * C) ** -0.5, 0.15625, ((0, 8),)),
        "output_weight": normal_values(splits[5], (SECTIONS, C, C), C ** -0.5, 0.5, ((0, 8),)),
    }


def denoise(previous, noise_part, noise_scale, spatial, temporal, out_weight):
    noisy = previous.astype(jnp.float32) + noise_scale * noise_part.astype(jnp.float32)
    normalized = (noisy * jax.lax.rsqrt(lax.optimization_barrier(jnp.mean(noisy * noisy, axis=-1, keepdims=True)) + 1e-05)).astype(jnp.bfloat16)
    bordered = jnp.pad(normalized, ((0, 0), (1, 1), (1, 1), (1, 1), (0, 0)))
    num_videos, num_frames, num_rows, num_cols, channels = previous.shape
    accumulated = jnp.zeros((num_videos * num_frames * num_rows * num_cols, channels), jnp.float32)
    for tap_index in range(9):
        row_offset = tap_index // 3
        col_offset = tap_index % 3
        shifted_view = bordered[:, 1:1 + num_frames, row_offset:row_offset + num_rows, col_offset:col_offset + num_cols, :]
        accumulated = accumulated + jnp.dot(shifted_view.reshape(-1, channels), spatial[tap_index], preferred_element_type=jnp.float32)
    for tap_index in range(3):
        shifted_view = bordered[:, tap_index:tap_index + num_frames, 1:1 + num_rows, 1:1 + num_cols, :]
        accumulated = accumulated + jnp.dot(shifted_view.reshape(-1, channels), temporal[tap_index], preferred_element_type=jnp.float32)
    activated = jax.nn.silu(accumulated).astype(jnp.bfloat16)
    estimate = jnp.dot(activated, out_weight, preferred_element_type=jnp.float32).reshape(previous.shape)
    return (noisy - noise_scale * estimate).astype(jnp.bfloat16)

def reference(base_frames, section_noise, noise_levels, spatial_kernel, temporal_kernel, output_weight):
    incoming = base_frames
    results = []
    for section_number in range(SECTIONS):
        level = noise_levels[section_number].astype(jnp.float32)
        produced = denoise(incoming, section_noise[section_number], level, spatial_kernel[section_number], temporal_kernel[section_number], output_weight[section_number])
        results.append(produced)
        incoming = produced
    return jnp.stack(results)
```

```python
import jax
import jax.numpy as jnp
from jax import lax
from jax.sharding import PartitionSpec as P


def shift_in(block, axis, dim):
    count = lax.axis_size(axis)
    forward = [(i, i + 1) for i in range(count - 1)]
    backward = [(i + 1, i) for i in range(count - 1)]
    size = block.shape[dim]
    low = lax.ppermute(lax.slice_in_dim(block, size - 1, size, axis=dim), axis, forward)
    high = lax.ppermute(lax.slice_in_dim(block, 0, 1, axis=dim), axis, backward)
    return low, high


def denoise(previous, noise_part, noise_scale, spatial, temporal, out_weight):
    noisy = previous.astype(jnp.float32) + noise_scale * noise_part.astype(jnp.float32)
    normalized = (
        noisy * lax.rsqrt(jnp.mean(noisy * noisy, axis=-1, keepdims=True) + 1e-05)
    ).astype(jnp.bfloat16)
    low_f, high_f = shift_in(normalized, "frames", 1)
    low_r, high_r = shift_in(normalized, "space", 2)
    rows_ext = jnp.concatenate([low_r, normalized, high_r], axis=2)
    rows_ext = jnp.pad(rows_ext, ((0, 0), (0, 0), (0, 0), (1, 1), (0, 0)))
    frames_ext = jnp.concatenate([low_f, normalized, high_f], axis=1)
    num_videos, num_frames, num_rows, num_cols, channels = previous.shape
    accumulated = jnp.zeros((num_videos * num_frames * num_rows * num_cols, channels), jnp.float32)
    for tap_index in range(9):
        row_offset = tap_index // 3
        col_offset = tap_index % 3
        shifted_view = rows_ext[
            :, :, row_offset : row_offset + num_rows, col_offset : col_offset + num_cols, :
        ]
        accumulated = accumulated + jnp.dot(
            shifted_view.reshape(-1, channels),
            spatial[tap_index],
            preferred_element_type=jnp.float32,
        )
    for tap_index in range(3):
        shifted_view = frames_ext[:, tap_index : tap_index + num_frames]
        accumulated = accumulated + jnp.dot(
            shifted_view.reshape(-1, channels),
            temporal[tap_index],
            preferred_element_type=jnp.float32,
        )
    activated = jax.nn.silu(accumulated).astype(jnp.bfloat16)
    estimate = jnp.dot(activated, out_weight, preferred_element_type=jnp.float32).reshape(
        previous.shape
    )
    return (noisy - noise_scale * estimate).astype(jnp.bfloat16)


def on_device(
    base_frames, section_noise, noise_levels, spatial_kernel, temporal_kernel, output_weight
):
    place = lax.axis_index("section")
    sections = lax.axis_size("section")
    video_count = base_frames.shape[0]
    per_device = video_count // sections
    noise_t = lax.all_to_all(section_noise[0], "section", 0, 0, tiled=True)
    noise_t = noise_t.reshape((sections, per_device) + noise_t.shape[1:])
    levels = lax.all_gather(noise_levels, "section", tiled=True)
    spatial = lax.all_gather(spatial_kernel, "section", tiled=True)
    temporal = lax.all_gather(temporal_kernel, "section", tiled=True)
    out_weight = lax.all_gather(output_weight, "section", tiled=True)
    incoming = lax.dynamic_slice_in_dim(base_frames, place * per_device, per_device, 0)
    results = []
    for k in range(sections):
        incoming = denoise(
            incoming,
            noise_t[k],
            levels[k].astype(jnp.float32),
            spatial[k],
            temporal[k],
            out_weight[k],
        )
        results.append(incoming)
    stacked = jnp.stack(results)
    return lax.all_to_all(stacked, "section", 0, 1, tiled=True)


def solution(mesh):
    return jax.shard_map(
        on_device,
        mesh=mesh,
        in_specs=(
            P(None, "frames", "space", None, None),
            P("section", None, "frames", "space", None, None),
            P("section"),
            P("section", None, None, None),
            P("section", None, None, None),
            P("section", None, None),
        ),
        out_specs=P("section", None, "frames", "space", None, None),
        check_vma=False,
    )
```

```python
import jax
import jax.numpy as jnp
from jax import lax
from jax.sharding import PartitionSpec as P


def shift_in(block, axis, dim):
    count = lax.axis_size(axis)
    forward = [(i, i + 1) for i in range(count - 1)]
    backward = [(i + 1, i) for i in range(count - 1)]
    size = block.shape[dim]
    low = lax.ppermute(lax.slice_in_dim(block, size - 1, size, axis=dim), axis, forward)
    high = lax.ppermute(lax.slice_in_dim(block, 0, 1, axis=dim), axis, backward)
    return low, high


def denoise(previous, noise_part, noise_scale, spatial, temporal, out_weight):
    noisy = previous.astype(jnp.float32) + noise_scale * noise_part.astype(jnp.float32)
    normalized = (
        noisy * lax.rsqrt(jnp.mean(noisy * noisy, axis=-1, keepdims=True) + 1e-05)
    ).astype(jnp.bfloat16)
    low_f, high_f = shift_in(normalized, "frames", 1)
    low_r, high_r = shift_in(normalized, "space", 2)
    rows_ext = jnp.concatenate([low_r, normalized, high_r], axis=2)
    rows_ext = jnp.pad(rows_ext, ((0, 0), (0, 0), (0, 0), (1, 1), (0, 0)))
    frames_ext = jnp.concatenate([low_f, normalized, high_f], axis=1)
    num_videos, num_frames, num_rows, num_cols, channels = previous.shape
    accumulated = jnp.zeros((num_videos * num_frames * num_rows * num_cols, channels), jnp.float32)
    for tap_index in range(9):
        row_offset = tap_index // 3
        col_offset = tap_index % 3
        shifted_view = rows_ext[
            :, :, row_offset : row_offset + num_rows, col_offset : col_offset + num_cols, :
        ]
        accumulated = accumulated + jnp.dot(
            shifted_view.reshape(-1, channels),
            spatial[tap_index],
            preferred_element_type=jnp.float32,
        )
    for tap_index in range(3):
        shifted_view = frames_ext[:, tap_index : tap_index + num_frames]
        accumulated = accumulated + jnp.dot(
            shifted_view.reshape(-1, channels),
            temporal[tap_index],
            preferred_element_type=jnp.float32,
        )
    activated = jax.nn.silu(accumulated).astype(jnp.bfloat16)
    estimate = jnp.dot(activated, out_weight, preferred_element_type=jnp.float32).reshape(
        previous.shape
    )
    return (noisy - noise_scale * estimate).astype(jnp.bfloat16)


def on_device(
    base_frames, section_noise, noise_levels, spatial_kernel, temporal_kernel, output_weight
):
    place = lax.axis_index("section")
    sections = lax.axis_size("section")
    video_count = base_frames.shape[0]
    per_device = video_count // sections
    noise_t = lax.all_to_all(section_noise[0], "section", 0, 0, tiled=True)
    noise_t = noise_t.reshape((sections, per_device) + noise_t.shape[1:])
    channels = spatial_kernel.shape[-1]
    level_slab = jnp.broadcast_to(
        noise_levels.reshape(1, 1, 1, 1), (1, 1, channels, channels)
    ).astype(spatial_kernel.dtype)
    packed = jnp.concatenate(
        [spatial_kernel, temporal_kernel, output_weight[:, None], level_slab], axis=1
    )
    packed = lax.all_gather(packed, "section", tiled=True)
    incoming = lax.dynamic_slice_in_dim(base_frames, place * per_device, per_device, 0)
    results = []
    for k in range(sections):
        incoming = denoise(
            incoming,
            noise_t[k],
            packed[k, 13, 0, 0].astype(jnp.float32),
            packed[k, 0:9],
            packed[k, 9:12],
            packed[k, 12],
        )
        results.append(incoming)
    stacked = jnp.stack(results)
    return lax.all_to_all(stacked, "section", 0, 1, tiled=True)


def solution(mesh):
    return jax.shard_map(
        on_device,
        mesh=mesh,
        in_specs=(
            P(None, "frames", "space", None, None),
            P("section", None, "frames", "space", None, None),
            P("section"),
            P("section", None, None, None),
            P("section", None, None, None),
            P("section", None, None),
        ),
        out_specs=P("section", None, "frames", "space", None, None),
        check_vma=False,
    )
```

```python
import jax
import jax.numpy as jnp
from jax import lax
from jax.sharding import PartitionSpec as P

HALO = 4


def extend(block, width, frame_dim, row_dim):
    for axis, dim in (("frames", frame_dim), ("space", row_dim)):
        count = lax.axis_size(axis)
        forward = [(i, i + 1) for i in range(count - 1)]
        backward = [(i + 1, i) for i in range(count - 1)]
        size = block.shape[dim]
        low = lax.ppermute(lax.slice_in_dim(block, size - width, size, axis=dim), axis, forward)
        high = lax.ppermute(lax.slice_in_dim(block, 0, width, axis=dim), axis, backward)
        block = jnp.concatenate([low, block, high], axis=dim)
    return block


def inside_mask(num_frames, num_rows, width):
    frame_place = lax.axis_index("frames")
    row_place = lax.axis_index("space")
    total_frames = num_frames * lax.axis_size("frames")
    total_rows = num_rows * lax.axis_size("space")
    frames = frame_place * num_frames - width + jnp.arange(num_frames + 2 * width)
    rows = row_place * num_rows - width + jnp.arange(num_rows + 2 * width)
    frame_ok = (frames >= 0) & (frames < total_frames)
    row_ok = (rows >= 0) & (rows < total_rows)
    return (frame_ok[:, None] & row_ok[None, :])[None, :, :, None, None]


def denoise(previous, noise_part, noise_scale, spatial, temporal, out_weight, mask):
    noisy = previous.astype(jnp.float32) + noise_scale * noise_part.astype(jnp.float32)
    normalized = (
        noisy * lax.rsqrt(jnp.mean(noisy * noisy, axis=-1, keepdims=True) + 1e-05)
    ).astype(jnp.bfloat16)
    normalized = jnp.where(mask, normalized, jnp.zeros_like(normalized))
    num_videos, m, n, num_cols, channels = previous.shape
    padded = jnp.pad(normalized, ((0, 0), (0, 0), (0, 0), (1, 1), (0, 0)))
    accumulated = jnp.zeros((num_videos * (m - 2) * (n - 2) * num_cols, channels), jnp.float32)
    for tap_index in range(9):
        row_offset = tap_index // 3
        col_offset = tap_index % 3
        shifted_view = padded[
            :, 1 : m - 1, row_offset : row_offset + n - 2, col_offset : col_offset + num_cols, :
        ]
        accumulated = accumulated + jnp.dot(
            shifted_view.reshape(-1, channels),
            spatial[tap_index],
            preferred_element_type=jnp.float32,
        )
    for tap_index in range(3):
        shifted_view = normalized[:, tap_index : tap_index + m - 2, 1 : n - 1]
        accumulated = accumulated + jnp.dot(
            shifted_view.reshape(-1, channels),
            temporal[tap_index],
            preferred_element_type=jnp.float32,
        )
    activated = jax.nn.silu(accumulated).astype(jnp.bfloat16)
    estimate = jnp.dot(activated, out_weight, preferred_element_type=jnp.float32).reshape(
        (num_videos, m - 2, n - 2, num_cols, channels)
    )
    return (noisy[:, 1 : m - 1, 1 : n - 1] - noise_scale * estimate).astype(jnp.bfloat16)


def on_device(
    base_frames, section_noise, noise_levels, spatial_kernel, temporal_kernel, output_weight
):
    place = lax.axis_index("section")
    sections = lax.axis_size("section")
    video_count, num_frames, num_rows = base_frames.shape[:3]
    per_device = video_count // sections
    halo = HALO
    noise_t = lax.all_to_all(section_noise[0], "section", 0, 0, tiled=True)
    noise_t = noise_t.reshape((sections, per_device) + noise_t.shape[1:])
    channels = spatial_kernel.shape[-1]
    level_slab = jnp.broadcast_to(
        noise_levels.reshape(1, 1, 1, 1), (1, 1, channels, channels)
    ).astype(spatial_kernel.dtype)
    packed = jnp.concatenate(
        [spatial_kernel, temporal_kernel, output_weight[:, None], level_slab], axis=1
    )
    packed = lax.all_gather(packed, "section", tiled=True)
    incoming = lax.dynamic_slice_in_dim(base_frames, place * per_device, per_device, 0)
    both = extend(jnp.concatenate([incoming[None], noise_t], axis=0), halo, 2, 3)
    prior_ext = both[0]
    noise_ext = both[1:]
    masks = [inside_mask(num_frames, num_rows, w) for w in range(halo + 1)]
    results = []
    for k in range(sections):
        j = k % halo
        if j == 0 and k > 0:
            prior_ext = extend(prior_ext, halo, 1, 2)
        width = halo - j
        cut = halo - width
        noise_here = noise_ext[
            k, :, cut : cut + num_frames + 2 * width, cut : cut + num_rows + 2 * width
        ]
        prior_ext = denoise(
            prior_ext,
            noise_here,
            packed[k, 13, 0, 0].astype(jnp.float32),
            packed[k, 0:9],
            packed[k, 9:12],
            packed[k, 12],
            masks[width],
        )
        inner = width - 1
        results.append(
            prior_ext[:, inner : inner + num_frames, inner : inner + num_rows]
        )
    stacked = jnp.stack(results)
    return lax.all_to_all(stacked, "section", 0, 1, tiled=True)


def solution(mesh):
    return jax.shard_map(
        on_device,
        mesh=mesh,
        in_specs=(
            P(None, "frames", "space", None, None),
            P("section", None, "frames", "space", None, None),
            P("section"),
            P("section", None, None, None),
            P("section", None, None, None),
            P("section", None, None),
        ),
        out_specs=P("section", None, "frames", "space", None, None),
        check_vma=False,
    )
```

```python
import jax
import jax.numpy as jnp
from jax import lax
from jax.sharding import PartitionSpec as P

HALO = 4


def extend(block, width, frame_dim, row_dim):
    for axis, dim in (("frames", frame_dim), ("space", row_dim)):
        count = lax.axis_size(axis)
        forward = [(i, i + 1) for i in range(count - 1)]
        backward = [(i + 1, i) for i in range(count - 1)]
        size = block.shape[dim]
        low = lax.ppermute(lax.slice_in_dim(block, size - width, size, axis=dim), axis, forward)
        high = lax.ppermute(lax.slice_in_dim(block, 0, width, axis=dim), axis, backward)
        block = jnp.concatenate([low, block, high], axis=dim)
    return block


def inside_mask(num_frames, num_rows, width):
    frame_place = lax.axis_index("frames")
    row_place = lax.axis_index("space")
    total_frames = num_frames * lax.axis_size("frames")
    total_rows = num_rows * lax.axis_size("space")
    frames = frame_place * num_frames - width + jnp.arange(num_frames + 2 * width)
    rows = row_place * num_rows - width + jnp.arange(num_rows + 2 * width)
    frame_ok = (frames >= 0) & (frames < total_frames)
    row_ok = (rows >= 0) & (rows < total_rows)
    return (frame_ok[:, None] & row_ok[None, :])[None, :, :, None, None]


def denoise(previous, noise_part, noise_scale, spatial, temporal, out_weight, mask):
    noisy = previous.astype(jnp.float32) + noise_scale * noise_part.astype(jnp.float32)
    normalized = (
        noisy * lax.rsqrt(jnp.mean(noisy * noisy, axis=-1, keepdims=True) + 1e-05)
    ).astype(jnp.bfloat16)
    normalized = jnp.where(mask, normalized, jnp.zeros_like(normalized))
    num_videos, m, n, num_cols, channels = previous.shape
    padded = jnp.pad(normalized, ((0, 0), (0, 0), (0, 0), (1, 1), (0, 0)))
    col_views = lax.optimization_barrier(
        (padded[:, :, :, 0:num_cols], padded[:, :, :, 2 : num_cols + 2])
    )
    col_views = (col_views[0], normalized, col_views[1])
    accumulated = jnp.zeros((num_videos * (m - 2) * (n - 2) * num_cols, channels), jnp.float32)
    for tap_index in range(9):
        row_offset = tap_index // 3
        col_offset = tap_index % 3
        shifted_view = col_views[col_offset][:, 1 : m - 1, row_offset : row_offset + n - 2]
        accumulated = accumulated + jnp.dot(
            shifted_view.reshape(-1, channels),
            spatial[tap_index],
            preferred_element_type=jnp.float32,
        )
    for tap_index in range(3):
        shifted_view = normalized[:, tap_index : tap_index + m - 2, 1 : n - 1]
        accumulated = accumulated + jnp.dot(
            shifted_view.reshape(-1, channels),
            temporal[tap_index],
            preferred_element_type=jnp.float32,
        )
    activated = jax.nn.silu(accumulated).astype(jnp.bfloat16)
    estimate = jnp.dot(activated, out_weight, preferred_element_type=jnp.float32).reshape(
        (num_videos, m - 2, n - 2, num_cols, channels)
    )
    return (noisy[:, 1 : m - 1, 1 : n - 1] - noise_scale * estimate).astype(jnp.bfloat16)


def on_device(
    base_frames, section_noise, noise_levels, spatial_kernel, temporal_kernel, output_weight
):
    place = lax.axis_index("section")
    sections = lax.axis_size("section")
    video_count, num_frames, num_rows = base_frames.shape[:3]
    per_device = video_count // sections
    halo = HALO
    noise_t = lax.all_to_all(section_noise[0], "section", 0, 0, tiled=True)
    noise_t = noise_t.reshape((sections, per_device) + noise_t.shape[1:])
    channels = spatial_kernel.shape[-1]
    level_slab = jnp.broadcast_to(
        noise_levels.reshape(1, 1, 1, 1), (1, 1, channels, channels)
    ).astype(spatial_kernel.dtype)
    packed = jnp.concatenate(
        [spatial_kernel, temporal_kernel, output_weight[:, None], level_slab], axis=1
    )
    packed = lax.all_gather(packed, "section", tiled=True)
    incoming = lax.dynamic_slice_in_dim(base_frames, place * per_device, per_device, 0)
    both = extend(jnp.concatenate([incoming[None], noise_t[:halo]], axis=0), halo, 2, 3)
    prior_ext = both[0]
    noise_parts = [both[1:]]
    for start in range(halo, sections, halo):
        noise_parts.append(extend(noise_t[start : start + halo], halo, 2, 3))
    noise_ext = jnp.concatenate(noise_parts, axis=0)
    masks = [inside_mask(num_frames, num_rows, w) for w in range(halo + 1)]
    results = []
    for k in range(sections):
        j = k % halo
        if j == 0 and k > 0:
            prior_ext = extend(prior_ext, halo, 1, 2)
        width = halo - j
        cut = halo - width
        noise_here = noise_ext[
            k, :, cut : cut + num_frames + 2 * width, cut : cut + num_rows + 2 * width
        ]
        prior_ext = denoise(
            prior_ext,
            noise_here,
            packed[k, 13, 0, 0].astype(jnp.float32),
            packed[k, 0:9],
            packed[k, 9:12],
            packed[k, 12],
            masks[width],
        )
        inner = width - 1
        results.append(
            prior_ext[:, inner : inner + num_frames, inner : inner + num_rows]
        )
    stacked = jnp.stack(results)
    return lax.all_to_all(stacked, "section", 0, 1, tiled=True)


def solution(mesh):
    return jax.shard_map(
        on_device,
        mesh=mesh,
        in_specs=(
            P(None, "frames", "space", None, None),
            P("section", None, "frames", "space", None, None),
            P("section"),
            P("section", None, None, None),
            P("section", None, None, None),
            P("section", None, None),
        ),
        out_specs=P("section", None, "frames", "space", None, None),
        check_vma=False,
    )
```

```python
import jax
import jax.numpy as jnp
from jax import lax
import functools
from jax.experimental import pallas as pl
from jax.experimental.pallas import tpu as pltpu
from jax.sharding import PartitionSpec as P
from jax.experimental import pallas as pl
from jax.experimental.pallas import tpu as pltpu


def conv_kernel(m, n, cols, xl_ref, xc_ref, xr_ref, noisy_ref, w_ref, lv_ref, out_ref):
    channels = w_ref.shape[-1]
    rows_out = (m - 2) * (n - 2) * cols
    views = (xl_ref, xc_ref, xr_ref)
    acc = jnp.zeros((rows_out, channels), jnp.float32)
    for tap in range(9):
        a, b = tap // 3, tap % 3
        v = views[b][pl.ds(1, m - 2), pl.ds(a * cols, (n - 2) * cols), :]
        v = v.reshape(rows_out, channels).astype(jnp.bfloat16)
        acc = acc + jnp.dot(v, w_ref[tap], preferred_element_type=jnp.float32)
    for t in range(3):
        v = xc_ref[pl.ds(t, m - 2), pl.ds(cols, (n - 2) * cols), :]
        v = v.reshape(rows_out, channels).astype(jnp.bfloat16)
        acc = acc + jnp.dot(v, w_ref[9 + t], preferred_element_type=jnp.float32)
    act = (acc / (1.0 + jnp.exp(-acc))).astype(jnp.bfloat16)
    est = jnp.dot(act, w_ref[12], preferred_element_type=jnp.float32)
    noisy = noisy_ref[pl.ds(1, m - 2), pl.ds(cols, (n - 2) * cols), :].reshape(rows_out, channels)
    level = lv_ref[0:1, :]
    out_ref[...] = (noisy - level * est).astype(out_ref.dtype)


def conv_call(xl, xc, xr, noisy, weights, level_row, m, n, cols):
    channels = weights.shape[-1]
    rows_out = (m - 2) * (n - 2) * cols
    flops = 2 * rows_out * channels * channels * 13
    nbytes = 4 * 4 * m * n * cols * channels + 2 * 13 * channels * channels + 2 * rows_out * channels
    return pl.pallas_call(
        functools.partial(conv_kernel, m, n, cols),
        out_shape=jax.ShapeDtypeStruct((rows_out, channels), jnp.bfloat16),
        in_specs=[pl.BlockSpec(memory_space=pltpu.VMEM)] * 6,
        out_specs=pl.BlockSpec(memory_space=pltpu.VMEM),
        cost_estimate=pl.CostEstimate(flops=flops, bytes_accessed=nbytes, transcendentals=rows_out * channels),
    )(xl, xc, xr, noisy, weights, level_row)

HALO = 4


def extend(block, width, frame_dim, row_dim):
    for axis, dim in (("frames", frame_dim), ("space", row_dim)):
        count = lax.axis_size(axis)
        forward = [(i, i + 1) for i in range(count - 1)]
        backward = [(i + 1, i) for i in range(count - 1)]
        size = block.shape[dim]
        low = lax.ppermute(lax.slice_in_dim(block, size - width, size, axis=dim), axis, forward)
        high = lax.ppermute(lax.slice_in_dim(block, 0, width, axis=dim), axis, backward)
        block = jnp.concatenate([low, block, high], axis=dim)
    return block


def inside_mask(num_frames, num_rows, width):
    frame_place = lax.axis_index("frames")
    row_place = lax.axis_index("space")
    total_frames = num_frames * lax.axis_size("frames")
    total_rows = num_rows * lax.axis_size("space")
    frames = frame_place * num_frames - width + jnp.arange(num_frames + 2 * width)
    rows = row_place * num_rows - width + jnp.arange(num_rows + 2 * width)
    frame_ok = (frames >= 0) & (frames < total_frames)
    row_ok = (rows >= 0) & (rows < total_rows)
    return (frame_ok[:, None] & row_ok[None, :])[None, :, :, None, None]


def denoise(previous, noise_part, noise_scale, weights, mask):
    noisy = previous.astype(jnp.float32) + noise_scale * noise_part.astype(jnp.float32)
    normalized = (
        noisy * lax.rsqrt(jnp.mean(noisy * noisy, axis=-1, keepdims=True) + 1e-05)
    ).astype(jnp.bfloat16)
    normalized = jnp.where(mask, normalized, jnp.zeros_like(normalized))
    num_videos, m, n, num_cols, channels = previous.shape
    padded = jnp.pad(normalized, ((0, 0), (0, 0), (0, 0), (1, 1), (0, 0)))
    flat = lambda x: x.astype(jnp.float32).reshape(m, n * num_cols, channels)
    level_row = jnp.full((8, channels), noise_scale, jnp.float32)
    outs = []
    for v in range(num_videos):
        out = conv_call(
            flat(padded[v, :, :, 0:num_cols]),
            flat(normalized[v]),
            flat(padded[v, :, :, 2 : num_cols + 2]),
            noisy[v].reshape(m, n * num_cols, channels),
            weights,
            level_row,
            m,
            n,
            num_cols,
        )
        outs.append(out.reshape(m - 2, n - 2, num_cols, channels))
    return jnp.stack(outs)


def on_device(
    base_frames, section_noise, noise_levels, spatial_kernel, temporal_kernel, output_weight
):
    place = lax.axis_index("section")
    sections = lax.axis_size("section")
    video_count, num_frames, num_rows = base_frames.shape[:3]
    per_device = video_count // sections
    halo = HALO
    noise_t = lax.all_to_all(section_noise[0], "section", 0, 0, tiled=True)
    noise_t = noise_t.reshape((sections, per_device) + noise_t.shape[1:])
    channels = spatial_kernel.shape[-1]
    level_slab = jnp.broadcast_to(
        noise_levels.reshape(1, 1, 1, 1), (1, 1, channels, channels)
    ).astype(spatial_kernel.dtype)
    packed = jnp.concatenate(
        [spatial_kernel, temporal_kernel, output_weight[:, None], level_slab], axis=1
    )
    packed = lax.all_gather(packed, "section", tiled=True)
    incoming = lax.dynamic_slice_in_dim(base_frames, place * per_device, per_device, 0)
    both = extend(jnp.concatenate([incoming[None], noise_t[:halo]], axis=0), halo, 2, 3)
    prior_ext = both[0]
    noise_parts = [both[1:]]
    for start in range(halo, sections, halo):
        noise_parts.append(extend(noise_t[start : start + halo], halo, 2, 3))
    noise_ext = jnp.concatenate(noise_parts, axis=0)
    masks = [inside_mask(num_frames, num_rows, w) for w in range(halo + 1)]
    results = []
    for k in range(sections):
        j = k % halo
        if j == 0 and k > 0:
            prior_ext = extend(prior_ext, halo, 1, 2)
        width = halo - j
        cut = halo - width
        noise_here = noise_ext[
            k, :, cut : cut + num_frames + 2 * width, cut : cut + num_rows + 2 * width
        ]
        prior_ext = denoise(
            prior_ext,
            noise_here,
            packed[k, 13, 0, 0].astype(jnp.float32),
            packed[k, 0:13],
            masks[width],
        )
        inner = width - 1
        results.append(
            prior_ext[:, inner : inner + num_frames, inner : inner + num_rows]
        )
    stacked = jnp.stack(results)
    return lax.all_to_all(stacked, "section", 0, 1, tiled=True)


def solution(mesh):
    return jax.shard_map(
        on_device,
        mesh=mesh,
        in_specs=(
            P(None, "frames", "space", None, None),
            P("section", None, "frames", "space", None, None),
            P("section"),
            P("section", None, None, None),
            P("section", None, None, None),
            P("section", None, None),
        ),
        out_specs=P("section", None, "frames", "space", None, None),
        check_vma=False,
    )
```

```python
import jax
import jax.numpy as jnp
from jax import lax
import functools
from jax.experimental import pallas as pl
from jax.experimental.pallas import tpu as pltpu
from jax.sharding import PartitionSpec as P

HALO = 4


def section_kernel(m, n, cols, prior_ref, noise_ref, mask_ref, w_ref, out_ref, xl, xc, xr, nz):
    channels = w_ref.shape[-1]
    rows_in = m * n * cols
    rows_out = (m - 2) * (n - 2) * cols
    level = w_ref[13][0:1, :].astype(jnp.float32)
    noisy = prior_ref[...].astype(jnp.float32) + level * noise_ref[...].astype(jnp.float32)
    mean_sq = jnp.mean(noisy * noisy, axis=-1, keepdims=True)
    normalized = (noisy * lax.rsqrt(mean_sq + 1e-05)).astype(jnp.bfloat16).astype(jnp.float32)
    normalized = jnp.where(mask_ref[...] > 0, normalized, 0.0)
    col = lax.broadcasted_iota(jnp.int32, (rows_in, channels), 0) % cols
    left = jnp.where(col == 0, 0.0, pltpu.roll(normalized, 1, 0))
    right = jnp.where(col == cols - 1, 0.0, pltpu.roll(normalized, rows_in - 1, 0))
    xl[...] = left.reshape(m, n * cols, channels)
    xc[...] = normalized.reshape(m, n * cols, channels)
    xr[...] = right.reshape(m, n * cols, channels)
    nz[...] = noisy.reshape(m, n * cols, channels)
    views = (xl, xc, xr)
    acc = jnp.zeros((rows_out, channels), jnp.float32)
    for tap in range(9):
        a, b = tap // 3, tap % 3
        v = views[b][pl.ds(1, m - 2), pl.ds(a * cols, (n - 2) * cols), :]
        v = v.reshape(rows_out, channels).astype(jnp.bfloat16)
        acc = acc + jnp.dot(v, w_ref[tap], preferred_element_type=jnp.float32)
    for t in range(3):
        v = xc[pl.ds(t, m - 2), pl.ds(cols, (n - 2) * cols), :]
        v = v.reshape(rows_out, channels).astype(jnp.bfloat16)
        acc = acc + jnp.dot(v, w_ref[9 + t], preferred_element_type=jnp.float32)
    act = (acc / (1.0 + jnp.exp(-acc))).astype(jnp.bfloat16)
    est = jnp.dot(act, w_ref[12], preferred_element_type=jnp.float32)
    inner = nz[pl.ds(1, m - 2), pl.ds(cols, (n - 2) * cols), :].reshape(rows_out, channels)
    out_ref[...] = (inner - level * est).astype(out_ref.dtype)


def section_call(prior, noise, mask, weights, m, n, cols):
    channels = weights.shape[-1]
    rows_in = m * n * cols
    rows_out = (m - 2) * (n - 2) * cols
    flops = 2 * rows_out * channels * channels * 13
    nbytes = 2 * 2 * rows_in * channels + 4 * rows_in * channels + 2 * 14 * channels * channels
    scratch = pltpu.VMEM((m, n * cols, channels), jnp.float32)
    return pl.pallas_call(
        functools.partial(section_kernel, m, n, cols),
        out_shape=jax.ShapeDtypeStruct((rows_out, channels), jnp.bfloat16),
        in_specs=[pl.BlockSpec(memory_space=pltpu.VMEM)] * 4,
        out_specs=pl.BlockSpec(memory_space=pltpu.VMEM),
        scratch_shapes=[scratch] * 4,
        cost_estimate=pl.CostEstimate(
            flops=flops, bytes_accessed=nbytes + 2 * rows_out * channels,
            transcendentals=rows_out * channels,
        ),
    )(prior, noise, mask, weights)


def extend(block, width, frame_dim, row_dim):
    for axis, dim in (("frames", frame_dim), ("space", row_dim)):
        count = lax.axis_size(axis)
        forward = [(i, i + 1) for i in range(count - 1)]
        backward = [(i + 1, i) for i in range(count - 1)]
        size = block.shape[dim]
        low = lax.ppermute(lax.slice_in_dim(block, size - width, size, axis=dim), axis, forward)
        high = lax.ppermute(lax.slice_in_dim(block, 0, width, axis=dim), axis, backward)
        block = jnp.concatenate([low, block, high], axis=dim)
    return block


def inside_mask(num_frames, num_rows, width):
    frame_place = lax.axis_index("frames")
    row_place = lax.axis_index("space")
    total_frames = num_frames * lax.axis_size("frames")
    total_rows = num_rows * lax.axis_size("space")
    frames = frame_place * num_frames - width + jnp.arange(num_frames + 2 * width)
    rows = row_place * num_rows - width + jnp.arange(num_rows + 2 * width)
    frame_ok = (frames >= 0) & (frames < total_frames)
    row_ok = (rows >= 0) & (rows < total_rows)
    return (frame_ok[:, None] & row_ok[None, :])[None, :, :, None, None]


def denoise(previous, noise_part, weights, mask):
    num_videos, m, n, num_cols, channels = previous.shape
    outs = []
    for v in range(num_videos):
        out = section_call(
            previous[v].reshape(-1, channels),
            noise_part[v].reshape(-1, channels),
            mask,
            weights,
            m,
            n,
            num_cols,
        )
        outs.append(out.reshape(m - 2, n - 2, num_cols, channels))
    return jnp.stack(outs)


def on_device(
    base_frames, section_noise, noise_levels, spatial_kernel, temporal_kernel, output_weight
):
    place = lax.axis_index("section")
    sections = lax.axis_size("section")
    video_count, num_frames, num_rows = base_frames.shape[:3]
    per_device = video_count // sections
    halo = HALO
    noise_t = lax.all_to_all(section_noise[0], "section", 0, 0, tiled=True)
    noise_t = noise_t.reshape((sections, per_device) + noise_t.shape[1:])
    channels = spatial_kernel.shape[-1]
    level_slab = jnp.broadcast_to(
        noise_levels.reshape(1, 1, 1, 1), (1, 1, channels, channels)
    ).astype(spatial_kernel.dtype)
    packed = jnp.concatenate(
        [spatial_kernel, temporal_kernel, output_weight[:, None], level_slab], axis=1
    )
    packed = lax.all_gather(packed, "section", tiled=True)
    incoming = lax.dynamic_slice_in_dim(base_frames, place * per_device, per_device, 0)
    both = extend(jnp.concatenate([incoming[None], noise_t[:halo]], axis=0), halo, 2, 3)
    prior_ext = both[0]
    noise_parts = [both[1:]]
    for start in range(halo, sections, halo):
        noise_parts.append(extend(noise_t[start : start + halo], halo, 2, 3))
    noise_ext = jnp.concatenate(noise_parts, axis=0)
    num_cols, channels = base_frames.shape[3:]
    masks = [
        jnp.broadcast_to(
            inside_mask(num_frames, num_rows, w)[0],
            (num_frames + 2 * w, num_rows + 2 * w, num_cols, channels),
        )
        .astype(jnp.float32)
        .reshape(-1, channels)
        for w in range(halo + 1)
    ]
    results = []
    for k in range(sections):
        j = k % halo
        if j == 0 and k > 0:
            prior_ext = extend(prior_ext, halo, 1, 2)
        width = halo - j
        cut = halo - width
        noise_here = noise_ext[
            k, :, cut : cut + num_frames + 2 * width, cut : cut + num_rows + 2 * width
        ]
        prior_ext = denoise(
            prior_ext,
            noise_here,
            packed[k],
            masks[width],
        )
        inner = width - 1
        results.append(
            prior_ext[:, inner : inner + num_frames, inner : inner + num_rows]
        )
    stacked = jnp.stack(results)
    return lax.all_to_all(stacked, "section", 0, 1, tiled=True)


def solution(mesh):
    return jax.shard_map(
        on_device,
        mesh=mesh,
        in_specs=(
            P(None, "frames", "space", None, None),
            P("section", None, "frames", "space", None, None),
            P("section"),
            P("section", None, None, None),
            P("section", None, None, None),
            P("section", None, None),
        ),
        out_specs=P("section", None, "frames", "space", None, None),
        check_vma=False,
    )
```

```python
import jax
import jax.numpy as jnp
from jax import lax
import functools
from jax.experimental import pallas as pl
from jax.experimental.pallas import tpu as pltpu
from jax.sharding import PartitionSpec as P

HALO = 4


def section_kernel(
    m, n, cols, inner, num_frames, num_rows,
    prior_ref, noise_ref, fm_ref, rm_ref, w_ref, out_ref, crop_ref, xl, xc, xr, nz,
):
    channels = w_ref.shape[-1]
    rows_in = m * n * cols
    rows_out = (m - 2) * (n - 2) * cols
    level = w_ref[13][0:1, :].astype(jnp.float32)
    noisy = prior_ref[...].astype(jnp.float32) + level * noise_ref[...].astype(jnp.float32)
    mean_sq = jnp.mean(noisy * noisy, axis=-1, keepdims=True)
    normalized = (noisy * lax.rsqrt(mean_sq + 1e-05)).astype(jnp.bfloat16).astype(jnp.float32)
    mask = fm_ref[...][:, 0:1, :] * rm_ref[...][None, :, :]
    normalized = jnp.where(mask > 0, normalized.reshape(m, n * cols, channels), 0.0)
    normalized = normalized.reshape(rows_in, channels)
    col = lax.broadcasted_iota(jnp.int32, (rows_in, channels), 0) % cols
    left = jnp.where(col == 0, 0.0, pltpu.roll(normalized, 1, 0))
    right = jnp.where(col == cols - 1, 0.0, pltpu.roll(normalized, rows_in - 1, 0))
    xl[...] = left.reshape(m, n * cols, channels)
    xc[...] = normalized.reshape(m, n * cols, channels)
    xr[...] = right.reshape(m, n * cols, channels)
    nz[...] = noisy.reshape(m, n * cols, channels)
    views = (xl, xc, xr)
    acc = jnp.zeros((rows_out, channels), jnp.float32)
    for tap in range(9):
        a, b = tap // 3, tap % 3
        v = views[b][pl.ds(1, m - 2), pl.ds(a * cols, (n - 2) * cols), :]
        v = v.reshape(rows_out, channels).astype(jnp.bfloat16)
        acc = acc + jnp.dot(v, w_ref[tap], preferred_element_type=jnp.float32)
    for t in range(3):
        v = xc[pl.ds(t, m - 2), pl.ds(cols, (n - 2) * cols), :]
        v = v.reshape(rows_out, channels).astype(jnp.bfloat16)
        acc = acc + jnp.dot(v, w_ref[9 + t], preferred_element_type=jnp.float32)
    act = (acc / (1.0 + jnp.exp(-acc))).astype(jnp.bfloat16)
    est = jnp.dot(act, w_ref[12], preferred_element_type=jnp.float32)
    center = nz[pl.ds(1, m - 2), pl.ds(cols, (n - 2) * cols), :].reshape(rows_out, channels)
    result = center - level * est
    out_ref[...] = result.astype(out_ref.dtype)
    nz[pl.ds(0, m - 2), pl.ds(0, (n - 2) * cols), :] = result.reshape(m - 2, (n - 2) * cols, channels)
    crop = nz[pl.ds(inner, num_frames), pl.ds(inner * cols, num_rows * cols), :]
    crop_ref[...] = crop.reshape(num_frames * num_rows * cols, channels).astype(crop_ref.dtype)


def section_call(prior, noise, frame_mask, row_mask, weights, m, n, cols, num_frames, num_rows):
    channels = weights.shape[-1]
    rows_in = m * n * cols
    rows_out = (m - 2) * (n - 2) * cols
    rows_crop = num_frames * num_rows * cols
    inner = (m - 2 - num_frames) // 2
    flops = 2 * rows_out * channels * channels * 13
    nbytes = 2 * 2 * rows_in * channels + 2 * 14 * channels * channels
    nbytes += 2 * (rows_out + rows_crop) * channels
    scratch = pltpu.VMEM((m, n * cols, channels), jnp.float32)
    return pl.pallas_call(
        functools.partial(section_kernel, m, n, cols, inner, num_frames, num_rows),
        out_shape=(
            jax.ShapeDtypeStruct((rows_out, channels), jnp.bfloat16),
            jax.ShapeDtypeStruct((rows_crop, channels), jnp.bfloat16),
        ),
        in_specs=[pl.BlockSpec(memory_space=pltpu.VMEM)] * 5,
        out_specs=(
            pl.BlockSpec(memory_space=pltpu.VMEM),
            pl.BlockSpec(memory_space=pltpu.VMEM),
        ),
        scratch_shapes=[scratch] * 4,
        cost_estimate=pl.CostEstimate(
            flops=flops, bytes_accessed=nbytes, transcendentals=rows_out * channels
        ),
    )(prior, noise, frame_mask, row_mask, weights)


def extend(block, width, frame_dim, row_dim):
    for axis, dim in (("frames", frame_dim), ("space", row_dim)):
        count = lax.axis_size(axis)
        forward = [(i, i + 1) for i in range(count - 1)]
        backward = [(i + 1, i) for i in range(count - 1)]
        size = block.shape[dim]
        low = lax.ppermute(lax.slice_in_dim(block, size - width, size, axis=dim), axis, forward)
        high = lax.ppermute(lax.slice_in_dim(block, 0, width, axis=dim), axis, backward)
        block = jnp.concatenate([low, block, high], axis=dim)
    return block


def inside_masks(num_frames, num_rows, num_cols, channels, width):
    frame_place = lax.axis_index("frames")
    row_place = lax.axis_index("space")
    total_frames = num_frames * lax.axis_size("frames")
    total_rows = num_rows * lax.axis_size("space")
    frames = frame_place * num_frames - width + jnp.arange(num_frames + 2 * width)
    rows = row_place * num_rows - width + jnp.arange(num_rows + 2 * width)
    frame_ok = ((frames >= 0) & (frames < total_frames)).astype(jnp.float32)
    row_ok = ((rows >= 0) & (rows < total_rows)).astype(jnp.float32)
    frame_mask = jnp.broadcast_to(frame_ok[:, None, None], (num_frames + 2 * width, 8, channels))
    row_mask = jnp.broadcast_to(
        row_ok[:, None, None], (num_rows + 2 * width, num_cols, channels)
    ).reshape(-1, channels)
    return frame_mask, row_mask


def denoise(previous, noise_part, weights, masks, num_frames, num_rows):
    num_videos, m, n, num_cols, channels = previous.shape
    outs = []
    crops = []
    for v in range(num_videos):
        out, crop = section_call(
            previous[v].reshape(-1, channels),
            noise_part[v].reshape(-1, channels),
            masks[0],
            masks[1],
            weights,
            m,
            n,
            num_cols,
            num_frames,
            num_rows,
        )
        outs.append(out.reshape(m - 2, n - 2, num_cols, channels))
        crops.append(crop)
    return jnp.stack(outs), jnp.stack(crops)


def on_device(
    base_frames, section_noise, noise_levels, spatial_kernel, temporal_kernel, output_weight
):
    place = lax.axis_index("section")
    sections = lax.axis_size("section")
    video_count, num_frames, num_rows = base_frames.shape[:3]
    per_device = video_count // sections
    halo = HALO
    noise_t = lax.all_to_all(section_noise[0], "section", 0, 0, tiled=True)
    noise_t = noise_t.reshape((sections, per_device) + noise_t.shape[1:])
    channels = spatial_kernel.shape[-1]
    level_slab = jnp.broadcast_to(
        noise_levels.reshape(1, 1, 1, 1), (1, 1, channels, channels)
    ).astype(spatial_kernel.dtype)
    packed = jnp.concatenate(
        [spatial_kernel, temporal_kernel, output_weight[:, None], level_slab], axis=1
    )
    packed = lax.all_gather(packed, "section", tiled=True)
    incoming = lax.dynamic_slice_in_dim(base_frames, place * per_device, per_device, 0)
    both = extend(jnp.concatenate([incoming[None], noise_t[:halo]], axis=0), halo, 2, 3)
    prior_ext = both[0]
    noise_parts = [both[1:]]
    for start in range(halo, sections, halo):
        noise_parts.append(extend(noise_t[start : start + halo], halo, 2, 3))
    noise_ext = jnp.concatenate(noise_parts, axis=0)
    num_cols, channels = base_frames.shape[3:]
    masks = [
        inside_masks(num_frames, num_rows, num_cols, channels, w) for w in range(halo + 1)
    ]
    results = []
    for k in range(sections):
        j = k % halo
        if j == 0 and k > 0:
            prior_ext = extend(prior_ext, halo, 1, 2)
        width = halo - j
        cut = halo - width
        noise_here = noise_ext[
            k, :, cut : cut + num_frames + 2 * width, cut : cut + num_rows + 2 * width
        ]
        prior_ext, crop = denoise(
            prior_ext, noise_here, packed[k], masks[width], num_frames, num_rows
        )
        results.append(crop)
    stacked = jnp.stack(results).reshape(
        (sections, per_device, num_frames, num_rows, num_cols, channels)
    )
    return lax.all_to_all(stacked, "section", 0, 1, tiled=True)


def solution(mesh):
    return jax.shard_map(
        on_device,
        mesh=mesh,
        in_specs=(
            P(None, "frames", "space", None, None),
            P("section", None, "frames", "space", None, None),
            P("section"),
            P("section", None, None, None),
            P("section", None, None, None),
            P("section", None, None),
        ),
        out_specs=P("section", None, "frames", "space", None, None),
        check_vma=False,
    )
```

```python
import jax
import jax.numpy as jnp
from jax import lax
import functools
from jax.experimental import pallas as pl
from jax.experimental.pallas import tpu as pltpu
from jax.sharding import PartitionSpec as P

HALO = 4


def section_kernel(
    m, n, cols, inner, num_frames, num_rows, total_frames, total_rows, k,
    offs_ref, lv_ref, prior_ref, noise_ref, w_hbm, out_ref, crop_ref, w_ref, sem, xl, xc, xr, nz,
):
    weight_copy = pltpu.make_async_copy(w_hbm.at[k], w_ref, sem)
    weight_copy.start()
    channels = w_ref.shape[-1]
    rows_in = m * n * cols
    rows_out = (m - 2) * (n - 2) * cols
    width = (m - num_frames) // 2
    level = lv_ref[k]
    noisy = prior_ref[...].astype(jnp.float32) + level * noise_ref[...].astype(jnp.float32)
    mean_sq = jnp.mean(noisy * noisy, axis=-1, keepdims=True)
    normalized = (noisy * lax.rsqrt(mean_sq + 1e-05)).astype(jnp.bfloat16).astype(jnp.float32)
    shape4 = (m, n, cols, channels)
    frame_at = offs_ref[0] - width + lax.broadcasted_iota(jnp.int32, shape4, 0)
    row_at = offs_ref[1] - width + lax.broadcasted_iota(jnp.int32, shape4, 1)
    inside = (frame_at >= 0) & (frame_at < total_frames) & (row_at >= 0) & (row_at < total_rows)
    inside = inside.reshape(m, n * cols, channels)
    normalized = jnp.where(inside, normalized.reshape(m, n * cols, channels), 0.0)
    normalized = normalized.reshape(rows_in, channels)
    col = lax.broadcasted_iota(jnp.int32, (rows_in, channels), 0) % cols
    left = jnp.where(col == 0, 0.0, pltpu.roll(normalized, 1, 0))
    right = jnp.where(col == cols - 1, 0.0, pltpu.roll(normalized, rows_in - 1, 0))
    xl[...] = left.reshape(m, n * cols, channels)
    xc[...] = normalized.reshape(m, n * cols, channels)
    xr[...] = right.reshape(m, n * cols, channels)
    nz[...] = noisy.reshape(m, n * cols, channels)
    weight_copy.wait()
    views = (xl, xc, xr)
    acc = jnp.zeros((rows_out, channels), jnp.float32)
    for tap in range(9):
        a, b = tap // 3, tap % 3
        v = views[b][pl.ds(1, m - 2), pl.ds(a * cols, (n - 2) * cols), :]
        v = v.reshape(rows_out, channels).astype(jnp.bfloat16)
        acc = acc + jnp.dot(v, w_ref[tap], preferred_element_type=jnp.float32)
    for t in range(3):
        v = xc[pl.ds(t, m - 2), pl.ds(cols, (n - 2) * cols), :]
        v = v.reshape(rows_out, channels).astype(jnp.bfloat16)
        acc = acc + jnp.dot(v, w_ref[9 + t], preferred_element_type=jnp.float32)
    act = (acc / (1.0 + jnp.exp(-acc))).astype(jnp.bfloat16)
    est = jnp.dot(act, w_ref[12], preferred_element_type=jnp.float32)
    center = nz[pl.ds(1, m - 2), pl.ds(cols, (n - 2) * cols), :].reshape(rows_out, channels)
    result = center - level * est
    out_ref[...] = result.astype(out_ref.dtype)
    nz[pl.ds(0, m - 2), pl.ds(0, (n - 2) * cols), :] = result.reshape(m - 2, (n - 2) * cols, channels)
    crop = nz[pl.ds(inner, num_frames), pl.ds(inner * cols, num_rows * cols), :]
    crop_ref[...] = crop.reshape(num_frames * num_rows * cols, channels).astype(crop_ref.dtype)


def section_call(offs, levels, prior, noise, packed, k, m, n, cols, num_frames, num_rows, totals):
    channels = packed.shape[-1]
    rows_in = m * n * cols
    rows_out = (m - 2) * (n - 2) * cols
    rows_crop = num_frames * num_rows * cols
    inner = (m - 2 - num_frames) // 2
    flops = 2 * rows_out * channels * channels * 13
    nbytes = 2 * 2 * rows_in * channels + 2 * 13 * channels * channels
    nbytes += 2 * (rows_out + rows_crop) * channels
    scratch = pltpu.VMEM((m, n * cols, channels), jnp.float32)
    smem = pl.BlockSpec(memory_space=pltpu.SMEM)
    vmem = pl.BlockSpec(memory_space=pltpu.VMEM)
    return pl.pallas_call(
        functools.partial(
            section_kernel, m, n, cols, inner, num_frames, num_rows, totals[0], totals[1], k
        ),
        out_shape=(
            jax.ShapeDtypeStruct((rows_out, channels), jnp.bfloat16),
            jax.ShapeDtypeStruct((rows_crop, channels), jnp.bfloat16),
        ),
        in_specs=[smem, smem, vmem, vmem, pl.BlockSpec(memory_space=pl.ANY)],
        out_specs=(vmem, vmem),
        scratch_shapes=[
            pltpu.VMEM(packed.shape[1:], packed.dtype),
            pltpu.SemaphoreType.DMA(()),
        ]
        + [scratch] * 4,
        cost_estimate=pl.CostEstimate(
            flops=flops, bytes_accessed=nbytes, transcendentals=rows_out * channels
        ),
    )(offs, levels, prior, noise, packed)


def extend(block, width, frame_dim, row_dim):
    for axis, dim in (("frames", frame_dim), ("space", row_dim)):
        count = lax.axis_size(axis)
        forward = [(i, i + 1) for i in range(count - 1)]
        backward = [(i + 1, i) for i in range(count - 1)]
        size = block.shape[dim]
        low = lax.ppermute(lax.slice_in_dim(block, size - width, size, axis=dim), axis, forward)
        high = lax.ppermute(lax.slice_in_dim(block, 0, width, axis=dim), axis, backward)
        block = jnp.concatenate([low, block, high], axis=dim)
    return block


def denoise(offs, levels, previous, noise_part, packed, k, num_frames, num_rows, totals):
    num_videos, m, n, num_cols, channels = previous.shape
    outs = []
    crops = []
    for v in range(num_videos):
        out, crop = section_call(
            offs,
            levels,
            previous[v].reshape(-1, channels),
            noise_part[v].reshape(-1, channels),
            packed,
            k,
            m,
            n,
            num_cols,
            num_frames,
            num_rows,
            totals,
        )
        outs.append(out.reshape(m - 2, n - 2, num_cols, channels))
        crops.append(crop)
    return jnp.stack(outs), jnp.stack(crops)


def on_device(
    base_frames, section_noise, noise_levels, spatial_kernel, temporal_kernel, output_weight
):
    place = lax.axis_index("section")
    sections = lax.axis_size("section")
    video_count, num_frames, num_rows = base_frames.shape[:3]
    per_device = video_count // sections
    halo = HALO
    noise_t = lax.all_to_all(section_noise[0], "section", 0, 0, tiled=True)
    noise_t = noise_t.reshape((sections, per_device) + noise_t.shape[1:])
    channels = spatial_kernel.shape[-1]
    level_slab = jnp.broadcast_to(
        noise_levels.reshape(1, 1, 1, 1), (1, 1, channels, channels)
    ).astype(spatial_kernel.dtype)
    packed = jnp.concatenate(
        [spatial_kernel, temporal_kernel, output_weight[:, None], level_slab], axis=1
    )
    packed = lax.all_gather(packed, "section", tiled=True)
    incoming = lax.dynamic_slice_in_dim(base_frames, place * per_device, per_device, 0)
    levels = packed[:, 13, 0, 0].astype(jnp.float32)
    offs = jnp.stack(
        [lax.axis_index("frames") * num_frames, lax.axis_index("space") * num_rows]
    ).astype(jnp.int32)
    totals = (num_frames * lax.axis_size("frames"), num_rows * lax.axis_size("space"))
    both = extend(jnp.concatenate([incoming[None], noise_t[:halo]], axis=0), halo, 2, 3)
    prior_ext = both[0]
    noise_round = both[1:]
    results = []
    for k in range(sections):
        j = k % halo
        if j == 0 and k > 0:
            prior_ext = extend(prior_ext, halo, 1, 2)
            noise_round = noise_next
        width = halo - j
        cut = halo - width
        noise_here = noise_round[
            j, :, cut : cut + num_frames + 2 * width, cut : cut + num_rows + 2 * width
        ]
        prior_ext, crop = denoise(
            offs, levels, prior_ext, noise_here, packed, k, num_frames, num_rows, totals
        )
        results.append(crop)
        if j == 0 and k + halo < sections:
            later, _ = lax.optimization_barrier((noise_t[k + halo : k + 2 * halo], crop))
            noise_next = extend(later, halo, 2, 3)
    num_cols, channels = base_frames.shape[3:]
    stacked = jnp.stack(results).reshape(
        (sections, per_device, num_frames, num_rows, num_cols, channels)
    )
    return lax.all_to_all(stacked, "section", 0, 1, tiled=True)


def solution(mesh):
    return jax.shard_map(
        on_device,
        mesh=mesh,
        in_specs=(
            P(None, "frames", "space", None, None),
            P("section", None, "frames", "space", None, None),
            P("section"),
            P("section", None, None, None),
            P("section", None, None, None),
            P("section", None, None),
        ),
        out_specs=P("section", None, "frames", "space", None, None),
        check_vma=False,
    )
```

```python
import jax
import jax.numpy as jnp
from jax import lax
import functools
from jax.experimental import pallas as pl
from jax.experimental.pallas import tpu as pltpu
from jax.sharding import PartitionSpec as P

HALO = 4


def section_kernel(
    m, n, cols, inner, num_frames, num_rows, total_frames, total_rows, k,
    offs_ref, lv_ref, prior_ref, noise_ref, w_hbm, out_ref, crop_ref, w_ref, sem, xl, xc, xr, nz,
):
    weight_copy = pltpu.make_async_copy(w_hbm.at[k], w_ref, sem)
    weight_copy.start()
    channels = w_ref.shape[-1]
    rows_in = m * n * cols
    rows_out = (m - 2) * (n - 2) * cols
    width = (m - num_frames) // 2
    level = lv_ref[k]
    noisy = prior_ref[...].astype(jnp.float32) + level * noise_ref[...].astype(jnp.float32)
    mean_sq = jnp.mean(noisy * noisy, axis=-1, keepdims=True)
    normalized = (noisy * lax.rsqrt(mean_sq + 1e-05)).astype(jnp.bfloat16).astype(jnp.float32)
    shape4 = (m, n, cols, channels)
    frame_at = offs_ref[0] - width + lax.broadcasted_iota(jnp.int32, shape4, 0)
    row_at = offs_ref[1] - width + lax.broadcasted_iota(jnp.int32, shape4, 1)
    inside = (frame_at >= 0) & (frame_at < total_frames) & (row_at >= 0) & (row_at < total_rows)
    inside = inside.reshape(m, n * cols, channels)
    normalized = jnp.where(inside, normalized.reshape(m, n * cols, channels), 0.0)
    normalized = normalized.reshape(rows_in, channels)
    col = lax.broadcasted_iota(jnp.int32, (rows_in, channels), 0) % cols
    left = jnp.where(col == 0, 0.0, pltpu.roll(normalized, 1, 0))
    right = jnp.where(col == cols - 1, 0.0, pltpu.roll(normalized, rows_in - 1, 0))
    xl[...] = left.reshape(m, n * cols, channels)
    xc[...] = normalized.reshape(m, n * cols, channels)
    xr[...] = right.reshape(m, n * cols, channels)
    nz[...] = noisy.reshape(m, n * cols, channels)
    weight_copy.wait()
    views = (xl, xc, xr)
    acc = jnp.zeros((rows_out, channels), jnp.float32)
    for tap in range(9):
        a, b = tap // 3, tap % 3
        v = views[b][pl.ds(1, m - 2), pl.ds(a * cols, (n - 2) * cols), :]
        v = v.reshape(rows_out, channels).astype(jnp.bfloat16)
        acc = acc + jnp.dot(v, w_ref[tap], preferred_element_type=jnp.float32)
    for t in range(3):
        v = xc[pl.ds(t, m - 2), pl.ds(cols, (n - 2) * cols), :]
        v = v.reshape(rows_out, channels).astype(jnp.bfloat16)
        acc = acc + jnp.dot(v, w_ref[9 + t], preferred_element_type=jnp.float32)
    act = (acc / (1.0 + jnp.exp(-acc))).astype(jnp.bfloat16)
    est = jnp.dot(act, w_ref[12], preferred_element_type=jnp.float32)
    center = nz[pl.ds(1, m - 2), pl.ds(cols, (n - 2) * cols), :].reshape(rows_out, channels)
    result = center - level * est
    out_ref[...] = result.astype(out_ref.dtype)
    nz[pl.ds(0, m - 2), pl.ds(0, (n - 2) * cols), :] = result.reshape(m - 2, (n - 2) * cols, channels)
    crop = nz[pl.ds(inner, num_frames), pl.ds(inner * cols, num_rows * cols), :]
    crop_ref[...] = crop.reshape(num_frames * num_rows * cols, channels).astype(crop_ref.dtype)


def section_call(offs, levels, prior, noise, packed, k, m, n, cols, num_frames, num_rows, totals):
    channels = packed.shape[-1]
    rows_in = m * n * cols
    rows_out = (m - 2) * (n - 2) * cols
    rows_crop = num_frames * num_rows * cols
    inner = (m - 2 - num_frames) // 2
    flops = 2 * rows_out * channels * channels * 13
    nbytes = 2 * 2 * rows_in * channels + 2 * 13 * channels * channels
    nbytes += 2 * (rows_out + rows_crop) * channels
    scratch = pltpu.VMEM((m, n * cols, channels), jnp.float32)
    smem = pl.BlockSpec(memory_space=pltpu.SMEM)
    vmem = pl.BlockSpec(memory_space=pltpu.VMEM)
    return pl.pallas_call(
        functools.partial(
            section_kernel, m, n, cols, inner, num_frames, num_rows, totals[0], totals[1], k
        ),
        out_shape=(
            jax.ShapeDtypeStruct((rows_out, channels), jnp.bfloat16),
            jax.ShapeDtypeStruct((rows_crop, channels), jnp.bfloat16),
        ),
        in_specs=[smem, smem, vmem, vmem, pl.BlockSpec(memory_space=pl.ANY)],
        out_specs=(vmem, vmem),
        scratch_shapes=[
            pltpu.VMEM(packed.shape[1:], packed.dtype),
            pltpu.SemaphoreType.DMA(()),
        ]
        + [scratch] * 4,
        cost_estimate=pl.CostEstimate(
            flops=flops, bytes_accessed=nbytes, transcendentals=rows_out * channels
        ),
    )(offs, levels, prior, noise, packed)


def extend(block, width, frame_dim, row_dim):
    for axis, dim in (("frames", frame_dim), ("space", row_dim)):
        count = lax.axis_size(axis)
        forward = [(i, i + 1) for i in range(count - 1)]
        backward = [(i + 1, i) for i in range(count - 1)]
        size = block.shape[dim]
        low = lax.ppermute(lax.slice_in_dim(block, size - width, size, axis=dim), axis, forward)
        high = lax.ppermute(lax.slice_in_dim(block, 0, width, axis=dim), axis, backward)
        block = jnp.concatenate([low, block, high], axis=dim)
    return block


def extend_each(items, widths):
    for axis, dim in (("frames", 1), ("space", 2)):
        count = lax.axis_size(axis)
        forward = [(i, i + 1) for i in range(count - 1)]
        backward = [(i + 1, i) for i in range(count - 1)]
        lows, highs, sizes = [], [], []
        for item, width in zip(items, widths):
            size = item.shape[dim]
            low = lax.slice_in_dim(item, size - width, size, axis=dim)
            high = lax.slice_in_dim(item, 0, width, axis=dim)
            sizes.append(low.shape)
            lows.append(low.reshape((low.shape[0], -1) + low.shape[3:]))
            highs.append(high.reshape((high.shape[0], -1) + high.shape[3:]))
        got_low = lax.ppermute(jnp.concatenate(lows, axis=1), axis, forward)
        got_high = lax.ppermute(jnp.concatenate(highs, axis=1), axis, backward)
        grown = []
        offset = 0
        for item, shape in zip(items, sizes):
            length = shape[1] * shape[2]
            low = got_low[:, offset : offset + length].reshape(shape)
            high = got_high[:, offset : offset + length].reshape(shape)
            offset += length
            grown.append(jnp.concatenate([low, item, high], axis=dim))
        items = grown
    return items


def denoise(offs, levels, previous, noise_part, packed, k, num_frames, num_rows, totals):
    num_videos, m, n, num_cols, channels = previous.shape
    outs = []
    crops = []
    for v in range(num_videos):
        out, crop = section_call(
            offs,
            levels,
            previous[v].reshape(-1, channels),
            noise_part[v].reshape(-1, channels),
            packed,
            k,
            m,
            n,
            num_cols,
            num_frames,
            num_rows,
            totals,
        )
        outs.append(out.reshape(m - 2, n - 2, num_cols, channels))
        crops.append(crop)
    return jnp.stack(outs), jnp.stack(crops)


def on_device(
    base_frames, section_noise, noise_levels, spatial_kernel, temporal_kernel, output_weight
):
    place = lax.axis_index("section")
    sections = lax.axis_size("section")
    video_count, num_frames, num_rows = base_frames.shape[:3]
    per_device = video_count // sections
    halo = HALO
    noise_t = lax.all_to_all(section_noise[0], "section", 0, 0, tiled=True)
    noise_t = noise_t.reshape((sections, per_device) + noise_t.shape[1:])
    channels = spatial_kernel.shape[-1]
    level_slab = jnp.broadcast_to(
        noise_levels.reshape(1, 1, 1, 1), (1, 1, channels, channels)
    ).astype(spatial_kernel.dtype)
    packed = jnp.concatenate(
        [spatial_kernel, temporal_kernel, output_weight[:, None], level_slab], axis=1
    )
    packed = lax.all_gather(packed, "section", tiled=True)
    incoming = lax.dynamic_slice_in_dim(base_frames, place * per_device, per_device, 0)
    levels = packed[:, 13, 0, 0].astype(jnp.float32)
    offs = jnp.stack(
        [lax.axis_index("frames") * num_frames, lax.axis_index("space") * num_rows]
    ).astype(jnp.int32)
    totals = (num_frames * lax.axis_size("frames"), num_rows * lax.axis_size("space"))
    widths = [halo - k % halo for k in range(sections)]
    grown = extend_each([incoming] + [noise_t[k] for k in range(sections)], [halo] + widths)
    prior_ext = grown[0]
    noise_ext = grown[1:]
    results = []
    for k in range(sections):
        if k % halo == 0 and k > 0:
            prior_ext = extend(prior_ext, halo, 1, 2)
        prior_ext, crop = denoise(
            offs, levels, prior_ext, noise_ext[k], packed, k, num_frames, num_rows, totals
        )
        results.append(crop)
    num_cols, channels = base_frames.shape[3:]
    stacked = jnp.stack(results).reshape(
        (sections, per_device, num_frames, num_rows, num_cols, channels)
    )
    return lax.all_to_all(stacked, "section", 0, 1, tiled=True)


def solution(mesh):
    return jax.shard_map(
        on_device,
        mesh=mesh,
        in_specs=(
            P(None, "frames", "space", None, None),
            P("section", None, "frames", "space", None, None),
            P("section"),
            P("section", None, None, None),
            P("section", None, None, None),
            P("section", None, None),
        ),
        out_specs=P("section", None, "frames", "space", None, None),
        check_vma=False,
    )
```

```python
import jax
import jax.numpy as jnp
from jax import lax
import functools
from jax.experimental import pallas as pl
from jax.experimental.pallas import tpu as pltpu
from jax.sharding import PartitionSpec as P

HALO = 4


def section_kernel(
    m, n, cols, inner, num_frames, num_rows, total_frames, total_rows, k,
    offs_ref, prior_ref, noise_ref, w_hbm, out_ref, crop_ref, w_ref, sem, xs, nz,
):
    weight_copy = pltpu.make_async_copy(w_hbm.at[k], w_ref, sem)
    weight_copy.start()
    channels = w_ref.shape[-1]
    rows_in = m * n * cols
    rows_out = (m - 2) * (n - 2) * cols
    width = (m - num_frames) // 2
    prior = prior_ref[...].astype(jnp.float32)
    noise = noise_ref[...].astype(jnp.float32)
    weight_copy.wait()
    level = w_ref[13][0:1, :].astype(jnp.float32)
    noisy = prior + level * noise
    mean_sq = jnp.mean(noisy * noisy, axis=-1, keepdims=True)
    normalized = (noisy * lax.rsqrt(mean_sq + 1e-05)).astype(jnp.bfloat16).astype(jnp.float32)
    shape4 = (m, n, cols, channels)
    frame_at = offs_ref[0] - width + lax.broadcasted_iota(jnp.int32, shape4, 0)
    row_at = offs_ref[1] - width + lax.broadcasted_iota(jnp.int32, shape4, 1)
    inside = (frame_at >= 0) & (frame_at < total_frames) & (row_at >= 0) & (row_at < total_rows)
    inside = inside.reshape(m, n * cols, channels)
    normalized = jnp.where(inside, normalized.reshape(m, n * cols, channels), 0.0)
    normalized = normalized.reshape(rows_in, channels)
    col = lax.broadcasted_iota(jnp.int32, (rows_in, channels), 0) % cols
    left = jnp.where(col == 0, 0.0, pltpu.roll(normalized, 1, 0))
    right = jnp.where(col == cols - 1, 0.0, pltpu.roll(normalized, rows_in - 1, 0))
    xs[:, :, 0:channels] = left.reshape(m, n * cols, channels)
    xs[:, :, channels : 2 * channels] = normalized.reshape(m, n * cols, channels)
    xs[:, :, 2 * channels : 3 * channels] = right.reshape(m, n * cols, channels)
    nz[...] = noisy.reshape(m, n * cols, channels)
    acc = jnp.zeros((rows_out, channels), jnp.float32)
    for a in range(3):
        v = xs[pl.ds(1, m - 2), pl.ds(a * cols, (n - 2) * cols), :]
        v = v.reshape(rows_out, 3 * channels).astype(jnp.bfloat16)
        w = w_ref[pl.ds(3 * a, 3)].reshape(3 * channels, channels)
        acc = acc + jnp.dot(v, w, preferred_element_type=jnp.float32)
    frame_views = [
        xs[pl.ds(t, m - 2), pl.ds(cols, (n - 2) * cols), pl.ds(channels, channels)].reshape(
            rows_out, channels
        )
        for t in range(3)
    ]
    v = jnp.concatenate(frame_views, axis=1).astype(jnp.bfloat16)
    w = w_ref[pl.ds(9, 3)].reshape(3 * channels, channels)
    acc = acc + jnp.dot(v, w, preferred_element_type=jnp.float32)
    act = (acc / (1.0 + jnp.exp(-acc))).astype(jnp.bfloat16)
    est = jnp.dot(act, w_ref[12], preferred_element_type=jnp.float32)
    center = nz[pl.ds(1, m - 2), pl.ds(cols, (n - 2) * cols), :].reshape(rows_out, channels)
    result = center - level * est
    out_ref[...] = result.astype(out_ref.dtype)
    nz[pl.ds(0, m - 2), pl.ds(0, (n - 2) * cols), :] = result.reshape(m - 2, (n - 2) * cols, channels)
    crop = nz[pl.ds(inner, num_frames), pl.ds(inner * cols, num_rows * cols), :]
    crop_ref[...] = crop.reshape(num_frames * num_rows * cols, channels).astype(crop_ref.dtype)


def section_call(offs, prior, noise, packed, k, m, n, cols, num_frames, num_rows, totals):
    channels = packed.shape[-1]
    rows_in = m * n * cols
    rows_out = (m - 2) * (n - 2) * cols
    rows_crop = num_frames * num_rows * cols
    inner = (m - 2 - num_frames) // 2
    flops = 2 * rows_out * channels * channels * 13
    nbytes = 2 * 2 * rows_in * channels + 2 * 13 * channels * channels
    nbytes += 2 * (rows_out + rows_crop) * channels
    scratch = pltpu.VMEM((m, n * cols, channels), jnp.float32)
    smem = pl.BlockSpec(memory_space=pltpu.SMEM)
    vmem = pl.BlockSpec(memory_space=pltpu.VMEM)
    return pl.pallas_call(
        functools.partial(
            section_kernel, m, n, cols, inner, num_frames, num_rows, totals[0], totals[1], k
        ),
        out_shape=(
            jax.ShapeDtypeStruct((rows_out, channels), jnp.bfloat16),
            jax.ShapeDtypeStruct((rows_crop, channels), jnp.bfloat16),
        ),
        in_specs=[smem, vmem, vmem, pl.BlockSpec(memory_space=pl.ANY)],
        out_specs=(vmem, vmem),
        scratch_shapes=[
            pltpu.VMEM(packed.shape[1:], packed.dtype),
            pltpu.SemaphoreType.DMA(()),
        ]
        + [pltpu.VMEM((m, n * cols, 3 * channels), jnp.float32), scratch],
        cost_estimate=pl.CostEstimate(
            flops=flops, bytes_accessed=nbytes, transcendentals=rows_out * channels
        ),
    )(offs, prior, noise, packed)


def extend(block, width, frame_dim, row_dim):
    for axis, dim in (("frames", frame_dim), ("space", row_dim)):
        count = lax.axis_size(axis)
        forward = [(i, i + 1) for i in range(count - 1)]
        backward = [(i + 1, i) for i in range(count - 1)]
        size = block.shape[dim]
        low = lax.ppermute(lax.slice_in_dim(block, size - width, size, axis=dim), axis, forward)
        high = lax.ppermute(lax.slice_in_dim(block, 0, width, axis=dim), axis, backward)
        block = jnp.concatenate([low, block, high], axis=dim)
    return block


def denoise(offs, previous, noise_part, packed, k, num_frames, num_rows, totals):
    num_videos, m, n, num_cols, channels = previous.shape
    outs = []
    crops = []
    for v in range(num_videos):
        out, crop = section_call(
            offs,
            previous[v].reshape(-1, channels),
            noise_part[v].reshape(-1, channels),
            packed,
            k,
            m,
            n,
            num_cols,
            num_frames,
            num_rows,
            totals,
        )
        outs.append(out.reshape(m - 2, n - 2, num_cols, channels))
        crops.append(crop)
    return jnp.stack(outs), jnp.stack(crops)


def on_device(
    base_frames, section_noise, noise_levels, spatial_kernel, temporal_kernel, output_weight
):
    place = lax.axis_index("section")
    sections = lax.axis_size("section")
    video_count, num_frames, num_rows = base_frames.shape[:3]
    per_device = video_count // sections
    halo = HALO
    noise_t = lax.all_to_all(section_noise[0], "section", 0, 0, tiled=True)
    noise_t = noise_t.reshape((sections, per_device) + noise_t.shape[1:])
    channels = spatial_kernel.shape[-1]
    level_slab = jnp.broadcast_to(
        noise_levels.reshape(1, 1, 1, 1), (1, 1, channels, channels)
    ).astype(spatial_kernel.dtype)
    packed = jnp.concatenate(
        [spatial_kernel, temporal_kernel, output_weight[:, None], level_slab], axis=1
    )
    packed = lax.all_gather(packed, "section", tiled=True)
    incoming = lax.dynamic_slice_in_dim(base_frames, place * per_device, per_device, 0)
    offs = jnp.stack(
        [lax.axis_index("frames") * num_frames, lax.axis_index("space") * num_rows]
    ).astype(jnp.int32)
    totals = (num_frames * lax.axis_size("frames"), num_rows * lax.axis_size("space"))
    both = extend(jnp.concatenate([incoming[None], noise_t[:halo]], axis=0), halo, 2, 3)
    prior_ext = both[0]
    noise_round = both[1:]
    results = []
    for k in range(sections):
        j = k % halo
        if j == 0 and k > 0:
            prior_ext = extend(prior_ext, halo, 1, 2)
            noise_round = noise_next
        width = halo - j
        cut = halo - width
        noise_here = noise_round[
            j, :, cut : cut + num_frames + 2 * width, cut : cut + num_rows + 2 * width
        ]
        prior_ext, crop = denoise(
            offs, prior_ext, noise_here, packed, k, num_frames, num_rows, totals
        )
        results.append(crop)
        if j == 0 and k + halo < sections:
            later, _ = lax.optimization_barrier((noise_t[k + halo : k + 2 * halo], crop))
            noise_next = extend(later, halo, 2, 3)
    num_cols, channels = base_frames.shape[3:]
    stacked = jnp.stack(results).reshape(
        (sections, per_device, num_frames, num_rows, num_cols, channels)
    )
    return lax.all_to_all(stacked, "section", 0, 1, tiled=True)


def solution(mesh):
    return jax.shard_map(
        on_device,
        mesh=mesh,
        in_specs=(
            P(None, "frames", "space", None, None),
            P("section", None, "frames", "space", None, None),
            P("section"),
            P("section", None, None, None),
            P("section", None, None, None),
            P("section", None, None),
        ),
        out_specs=P("section", None, "frames", "space", None, None),
        check_vma=False,
    )
```

```python
import jax
import jax.numpy as jnp
from jax import lax
import functools
from jax.experimental import pallas as pl
from jax.experimental.pallas import tpu as pltpu
from jax.sharding import PartitionSpec as P

HALO = 4


def section_kernel(
    m, n, cols, inner, num_frames, num_rows, total_frames, total_rows, k,
    offs_ref, prior_ref, noise_ref, w_hbm, out_ref, crop_ref, w_ref, sem, xs, nz,
):
    weight_copy = pltpu.make_async_copy(w_hbm.at[k], w_ref, sem)
    weight_copy.start()
    channels = w_ref.shape[-1]
    rows_in = m * n * cols
    rows_out = (m - 2) * (n - 2) * cols
    width = (m - num_frames) // 2
    prior = prior_ref[...].astype(jnp.float32)
    noise = noise_ref[...].astype(jnp.float32)
    weight_copy.wait()
    level = w_ref[13][0:1, :].astype(jnp.float32)
    noisy = prior + level * noise
    mean_sq = jnp.mean(noisy * noisy, axis=-1, keepdims=True)
    normalized = (noisy * lax.rsqrt(mean_sq + 1e-05)).astype(jnp.bfloat16).astype(jnp.float32)
    shape4 = (m, n, cols, channels)
    frame_at = offs_ref[0] - width + lax.broadcasted_iota(jnp.int32, shape4, 0)
    row_at = offs_ref[1] - width + lax.broadcasted_iota(jnp.int32, shape4, 1)
    inside = (frame_at >= 0) & (frame_at < total_frames) & (row_at >= 0) & (row_at < total_rows)
    inside = inside.reshape(m, n * cols, channels)
    normalized = jnp.where(inside, normalized.reshape(m, n * cols, channels), 0.0)
    normalized = normalized.reshape(rows_in, channels)
    col = lax.broadcasted_iota(jnp.int32, (rows_in, channels), 0) % cols
    left = jnp.where(col == 0, 0.0, pltpu.roll(normalized, 1, 0))
    right = jnp.where(col == cols - 1, 0.0, pltpu.roll(normalized, rows_in - 1, 0))
    xs[:, :, 0:channels] = left.reshape(m, n * cols, channels)
    xs[:, :, channels : 2 * channels] = normalized.reshape(m, n * cols, channels)
    xs[:, :, 2 * channels : 3 * channels] = right.reshape(m, n * cols, channels)
    nz[...] = noisy.reshape(m, n * cols, channels)
    acc = jnp.zeros((rows_out, channels), jnp.float32)
    for a in range(3):
        v = xs[pl.ds(1, m - 2), pl.ds(a * cols, (n - 2) * cols), :]
        v = v.reshape(rows_out, 3 * channels).astype(jnp.bfloat16)
        w = w_ref[pl.ds(3 * a, 3)].reshape(3 * channels, channels)
        acc = acc + jnp.dot(v, w, preferred_element_type=jnp.float32)
    frame_views = [
        xs[pl.ds(t, m - 2), pl.ds(cols, (n - 2) * cols), pl.ds(channels, channels)].reshape(
            rows_out, channels
        )
        for t in range(3)
    ]
    v = jnp.concatenate(frame_views, axis=1).astype(jnp.bfloat16)
    w = w_ref[pl.ds(9, 3)].reshape(3 * channels, channels)
    acc = acc + jnp.dot(v, w, preferred_element_type=jnp.float32)
    act = (acc / (1.0 + jnp.exp(-acc))).astype(jnp.bfloat16)
    est = jnp.dot(act, w_ref[12], preferred_element_type=jnp.float32)
    center = nz[pl.ds(1, m - 2), pl.ds(cols, (n - 2) * cols), :].reshape(rows_out, channels)
    result = center - level * est
    out_ref[...] = result.astype(out_ref.dtype)
    nz[pl.ds(0, m - 2), pl.ds(0, (n - 2) * cols), :] = result.reshape(m - 2, (n - 2) * cols, channels)
    crop = nz[pl.ds(inner, num_frames), pl.ds(inner * cols, num_rows * cols), :]
    crop_ref[...] = crop.reshape(num_frames * num_rows * cols, channels).astype(crop_ref.dtype)


def section_call(offs, prior, noise, packed, k, m, n, cols, num_frames, num_rows, totals):
    channels = packed.shape[-1]
    rows_in = m * n * cols
    rows_out = (m - 2) * (n - 2) * cols
    rows_crop = num_frames * num_rows * cols
    inner = (m - 2 - num_frames) // 2
    flops = 2 * rows_out * channels * channels * 13
    nbytes = 2 * 2 * rows_in * channels + 2 * 13 * channels * channels
    nbytes += 2 * (rows_out + rows_crop) * channels
    scratch = pltpu.VMEM((m, n * cols, channels), jnp.float32)
    smem = pl.BlockSpec(memory_space=pltpu.SMEM)
    vmem = pl.BlockSpec(memory_space=pltpu.VMEM)
    return pl.pallas_call(
        functools.partial(
            section_kernel, m, n, cols, inner, num_frames, num_rows, totals[0], totals[1], k
        ),
        out_shape=(
            jax.ShapeDtypeStruct((rows_out, channels), jnp.bfloat16),
            jax.ShapeDtypeStruct((rows_crop, channels), jnp.bfloat16),
        ),
        in_specs=[smem, vmem, vmem, pl.BlockSpec(memory_space=pl.ANY)],
        out_specs=(vmem, vmem),
        scratch_shapes=[
            pltpu.VMEM(packed.shape[1:], packed.dtype),
            pltpu.SemaphoreType.DMA(()),
        ]
        + [pltpu.VMEM((m, n * cols, 3 * channels), jnp.float32), scratch],
        cost_estimate=pl.CostEstimate(
            flops=flops, bytes_accessed=nbytes, transcendentals=rows_out * channels
        ),
    )(offs, prior, noise, packed)


def extend(block, width, frame_dim, row_dim):
    frames_count = lax.axis_size("frames")
    space_count = lax.axis_size("space")
    num_frames = block.shape[frame_dim]
    num_rows = block.shape[row_dim]

    def cut(x, f0, f1, r0, r1):
        x = lax.slice_in_dim(x, f0, f1, axis=frame_dim)
        return lax.slice_in_dim(x, r0, r1, axis=row_dim)

    def send(piece, df, dr):
        if dr == 0:
            pairs = [(i, i + df) for i in range(frames_count) if 0 <= i + df < frames_count]
            return lax.ppermute(piece, "frames", pairs)
        if df == 0:
            pairs = [(i, i + dr) for i in range(space_count) if 0 <= i + dr < space_count]
            return lax.ppermute(piece, "space", pairs)
        pairs = []
        for f in range(frames_count):
            for r in range(space_count):
                if 0 <= f + df < frames_count and 0 <= r + dr < space_count:
                    pairs.append((f * space_count + r, (f + df) * space_count + r + dr))
        return lax.ppermute(piece, ("frames", "space"), pairs)

    w = width
    lo_f, hi_f = (num_frames - w, num_frames), (0, w)
    lo_r, hi_r = (num_rows - w, num_rows), (0, w)
    all_f, all_r = (0, num_frames), (0, num_rows)
    grid = {}
    for sf, (src_f, df) in enumerate(((lo_f, 1), (all_f, 0), (hi_f, -1))):
        for sr, (src_r, dr) in enumerate(((lo_r, 1), (all_r, 0), (hi_r, -1))):
            if df == 0 and dr == 0:
                grid[sf, sr] = block
            else:
                grid[sf, sr] = send(cut(block, *src_f, *src_r), df, dr)
    bands = [
        jnp.concatenate([grid[sf, 0], grid[sf, 1], grid[sf, 2]], axis=row_dim) for sf in range(3)
    ]
    return jnp.concatenate(bands, axis=frame_dim)


def denoise(offs, previous, noise_part, packed, k, num_frames, num_rows, totals):
    num_videos, m, n, num_cols, channels = previous.shape
    outs = []
    crops = []
    for v in range(num_videos):
        out, crop = section_call(
            offs,
            previous[v].reshape(-1, channels),
            noise_part[v].reshape(-1, channels),
            packed,
            k,
            m,
            n,
            num_cols,
            num_frames,
            num_rows,
            totals,
        )
        outs.append(out.reshape(m - 2, n - 2, num_cols, channels))
        crops.append(crop)
    return jnp.stack(outs), jnp.stack(crops)


def on_device(
    base_frames, section_noise, noise_levels, spatial_kernel, temporal_kernel, output_weight
):
    place = lax.axis_index("section")
    sections = lax.axis_size("section")
    video_count, num_frames, num_rows = base_frames.shape[:3]
    per_device = video_count // sections
    halo = HALO
    noise_t = lax.all_to_all(section_noise[0], "section", 0, 0, tiled=True)
    noise_t = noise_t.reshape((sections, per_device) + noise_t.shape[1:])
    channels = spatial_kernel.shape[-1]
    level_slab = jnp.broadcast_to(
        noise_levels.reshape(1, 1, 1, 1), (1, 1, channels, channels)
    ).astype(spatial_kernel.dtype)
    packed = jnp.concatenate(
        [spatial_kernel, temporal_kernel, output_weight[:, None], level_slab], axis=1
    )
    packed = lax.all_gather(packed, "section", tiled=True)
    incoming = lax.dynamic_slice_in_dim(base_frames, place * per_device, per_device, 0)
    offs = jnp.stack(
        [lax.axis_index("frames") * num_frames, lax.axis_index("space") * num_rows]
    ).astype(jnp.int32)
    totals = (num_frames * lax.axis_size("frames"), num_rows * lax.axis_size("space"))
    both = extend(jnp.concatenate([incoming[None], noise_t[:halo]], axis=0), halo, 2, 3)
    prior_ext = both[0]
    noise_round = both[1:]
    results = []
    for k in range(sections):
        j = k % halo
        if j == 0 and k > 0:
            prior_ext = extend(prior_ext, halo, 1, 2)
            noise_round = noise_next
        width = halo - j
        cut = halo - width
        noise_here = noise_round[
            j, :, cut : cut + num_frames + 2 * width, cut : cut + num_rows + 2 * width
        ]
        prior_ext, crop = denoise(
            offs, prior_ext, noise_here, packed, k, num_frames, num_rows, totals
        )
        results.append(crop)
        if j == 0 and k + halo < sections:
            later, _ = lax.optimization_barrier((noise_t[k + halo : k + 2 * halo], crop))
            noise_next = extend(later, halo, 2, 3)
    num_cols, channels = base_frames.shape[3:]
    stacked = jnp.stack(results).reshape(
        (sections, per_device, num_frames, num_rows, num_cols, channels)
    )
    return lax.all_to_all(stacked, "section", 0, 1, tiled=True)


def solution(mesh):
    return jax.shard_map(
        on_device,
        mesh=mesh,
        in_specs=(
            P(None, "frames", "space", None, None),
            P("section", None, "frames", "space", None, None),
            P("section"),
            P("section", None, None, None),
            P("section", None, None, None),
            P("section", None, None),
        ),
        out_specs=P("section", None, "frames", "space", None, None),
        check_vma=False,
    )
```

```python
import jax
import jax.numpy as jnp
from jax import lax
import functools
from jax.experimental import pallas as pl
from jax.experimental.pallas import tpu as pltpu
from jax.sharding import PartitionSpec as P

HALO = 4


def section_kernel(
    m, n, cols, inner, num_frames, num_rows, total_frames, total_rows, k,
    offs_ref, lv_ref, prior_ref, noise_ref, w_hbm, out_ref, crop_ref, w_ref, sem, xl, xc, xr, nz,
):
    weight_copy = pltpu.make_async_copy(w_hbm.at[k], w_ref, sem)
    weight_copy.start()
    channels = w_ref.shape[-1]
    rows_in = m * n * cols
    rows_out = (m - 2) * (n - 2) * cols
    width = (m - num_frames) // 2
    level = lv_ref[k]
    noisy = prior_ref[...].astype(jnp.float32) + level * noise_ref[...].astype(jnp.float32)
    mean_sq = jnp.mean(noisy * noisy, axis=-1, keepdims=True)
    normalized = (noisy * lax.rsqrt(mean_sq + 1e-05)).astype(jnp.bfloat16).astype(jnp.float32)
    shape4 = (m, n, cols, channels)
    frame_at = offs_ref[0] - width + lax.broadcasted_iota(jnp.int32, shape4, 0)
    row_at = offs_ref[1] - width + lax.broadcasted_iota(jnp.int32, shape4, 1)
    inside = (frame_at >= 0) & (frame_at < total_frames) & (row_at >= 0) & (row_at < total_rows)
    inside = inside.reshape(m, n * cols, channels)
    normalized = jnp.where(inside, normalized.reshape(m, n * cols, channels), 0.0)
    normalized = normalized.reshape(rows_in, channels)
    col = lax.broadcasted_iota(jnp.int32, (rows_in, channels), 0) % cols
    left = jnp.where(col == 0, 0.0, pltpu.roll(normalized, 1, 0))
    right = jnp.where(col == cols - 1, 0.0, pltpu.roll(normalized, rows_in - 1, 0))
    xl[...] = left.reshape(m, n * cols, channels)
    xc[...] = normalized.reshape(m, n * cols, channels)
    xr[...] = right.reshape(m, n * cols, channels)
    nz[...] = noisy.reshape(m, n * cols, channels)
    weight_copy.wait()
    views = (xl, xc, xr)
    acc = jnp.zeros((rows_out, channels), jnp.float32)
    for tap in range(9):
        a, b = tap // 3, tap % 3
        v = views[b][pl.ds(1, m - 2), pl.ds(a * cols, (n - 2) * cols), :]
        v = v.reshape(rows_out, channels).astype(jnp.bfloat16)
        acc = acc + jnp.dot(v, w_ref[tap], preferred_element_type=jnp.float32)
    for t in range(3):
        v = xc[pl.ds(t, m - 2), pl.ds(cols, (n - 2) * cols), :]
        v = v.reshape(rows_out, channels).astype(jnp.bfloat16)
        acc = acc + jnp.dot(v, w_ref[9 + t], preferred_element_type=jnp.float32)
    act = (acc / (1.0 + jnp.exp(-acc))).astype(jnp.bfloat16)
    est = jnp.dot(act, w_ref[12], preferred_element_type=jnp.float32)
    center = nz[pl.ds(1, m - 2), pl.ds(cols, (n - 2) * cols), :].reshape(rows_out, channels)
    result = center - level * est
    out_ref[...] = result.astype(out_ref.dtype)
    nz[pl.ds(0, m - 2), pl.ds(0, (n - 2) * cols), :] = result.reshape(m - 2, (n - 2) * cols, channels)
    crop = nz[pl.ds(inner, num_frames), pl.ds(inner * cols, num_rows * cols), :]
    crop_ref[...] = crop.reshape(num_frames * num_rows * cols, channels).astype(crop_ref.dtype)


def section_call(offs, levels, prior, noise, packed, k, m, n, cols, num_frames, num_rows, totals):
    channels = packed.shape[-1]
    rows_in = m * n * cols
    rows_out = (m - 2) * (n - 2) * cols
    rows_crop = num_frames * num_rows * cols
    inner = (m - 2 - num_frames) // 2
    flops = 2 * rows_out * channels * channels * 13
    nbytes = 2 * 2 * rows_in * channels + 2 * 13 * channels * channels
    nbytes += 2 * (rows_out + rows_crop) * channels
    scratch = pltpu.VMEM((m, n * cols, channels), jnp.float32)
    smem = pl.BlockSpec(memory_space=pltpu.SMEM)
    vmem = pl.BlockSpec(memory_space=pltpu.VMEM)
    return pl.pallas_call(
        functools.partial(
            section_kernel, m, n, cols, inner, num_frames, num_rows, totals[0], totals[1], k
        ),
        out_shape=(
            jax.ShapeDtypeStruct((rows_out, channels), jnp.bfloat16),
            jax.ShapeDtypeStruct((rows_crop, channels), jnp.bfloat16),
        ),
        in_specs=[smem, smem, vmem, vmem, pl.BlockSpec(memory_space=pl.ANY)],
        out_specs=(vmem, vmem),
        scratch_shapes=[
            pltpu.VMEM(packed.shape[1:], packed.dtype),
            pltpu.SemaphoreType.DMA(()),
        ]
        + [scratch] * 4,
        cost_estimate=pl.CostEstimate(
            flops=flops, bytes_accessed=nbytes, transcendentals=rows_out * channels
        ),
    )(offs, levels, prior, noise, packed)


def extend(block, width, frame_dim, row_dim):
    for axis, dim in (("frames", frame_dim), ("space", row_dim)):
        count = lax.axis_size(axis)
        forward = [(i, i + 1) for i in range(count - 1)]
        backward = [(i + 1, i) for i in range(count - 1)]
        size = block.shape[dim]
        low = lax.ppermute(lax.slice_in_dim(block, size - width, size, axis=dim), axis, forward)
        high = lax.ppermute(lax.slice_in_dim(block, 0, width, axis=dim), axis, backward)
        block = jnp.concatenate([low, block, high], axis=dim)
    return block


def denoise(offs, levels, previous, noise_part, packed, k, num_frames, num_rows, totals):
    num_videos, m, n, num_cols, channels = previous.shape
    outs = []
    crops = []
    for v in range(num_videos):
        out, crop = section_call(
            offs,
            levels,
            previous[v].reshape(-1, channels),
            noise_part[v].reshape(-1, channels),
            packed,
            k,
            m,
            n,
            num_cols,
            num_frames,
            num_rows,
            totals,
        )
        outs.append(out.reshape(m - 2, n - 2, num_cols, channels))
        crops.append(crop)
    return jnp.stack(outs), jnp.stack(crops)


def on_device(
    base_frames, section_noise, noise_levels, spatial_kernel, temporal_kernel, output_weight
):
    place = lax.axis_index("section")
    sections = lax.axis_size("section")
    video_count, num_frames, num_rows = base_frames.shape[:3]
    per_device = video_count // sections
    halo = HALO
    noise_t = lax.all_to_all(section_noise[0], "section", 0, 0, tiled=True)
    noise_t = noise_t.reshape((sections, per_device) + noise_t.shape[1:])
    channels = spatial_kernel.shape[-1]
    level_slab = jnp.broadcast_to(
        noise_levels.reshape(1, 1, 1, 1), (1, 1, channels, channels)
    ).astype(spatial_kernel.dtype)
    packed = jnp.concatenate(
        [spatial_kernel, temporal_kernel, output_weight[:, None], level_slab], axis=1
    )
    packed = lax.all_gather(packed, "section", tiled=True)
    incoming = lax.dynamic_slice_in_dim(base_frames, place * per_device, per_device, 0)
    levels = packed[:, 13, 0, 0].astype(jnp.float32)
    offs = jnp.stack(
        [lax.axis_index("frames") * num_frames, lax.axis_index("space") * num_rows]
    ).astype(jnp.int32)
    totals = (num_frames * lax.axis_size("frames"), num_rows * lax.axis_size("space"))
    both = extend(jnp.concatenate([incoming[None], noise_t], axis=0), halo, 2, 3)
    prior_ext = both[0]
    noise_all = both[1:]
    results = []
    for k in range(sections):
        j = k % halo
        if j == 0 and k > 0:
            prior_ext = extend(prior_ext, halo, 1, 2)
        width = halo - j
        cut = halo - width
        noise_here = noise_all[
            k, :, cut : cut + num_frames + 2 * width, cut : cut + num_rows + 2 * width
        ]
        prior_ext, crop = denoise(
            offs, levels, prior_ext, noise_here, packed, k, num_frames, num_rows, totals
        )
        results.append(crop)
    num_cols, channels = base_frames.shape[3:]
    stacked = jnp.stack(results).reshape(
        (sections, per_device, num_frames, num_rows, num_cols, channels)
    )
    return lax.all_to_all(stacked, "section", 0, 1, tiled=True)


def solution(mesh):
    return jax.shard_map(
        on_device,
        mesh=mesh,
        in_specs=(
            P(None, "frames", "space", None, None),
            P("section", None, "frames", "space", None, None),
            P("section"),
            P("section", None, None, None),
            P("section", None, None, None),
            P("section", None, None),
        ),
        out_specs=P("section", None, "frames", "space", None, None),
        check_vma=False,
    )
```

```python
import jax
import jax.numpy as jnp
from jax import lax
import functools
from jax.experimental import pallas as pl
from jax.experimental.pallas import tpu as pltpu
from jax.sharding import PartitionSpec as P

HALO = 4


def section_kernel(
    m, n, cols, inner, num_frames, num_rows, total_frames, total_rows, k, j, cut,
    offs_ref, lv_ref, prior_ref, noise_hbm, w_hbm, out_ref, crop_ref,
    w_ref, sem, noise_raw, noise_sem, noise_wide, xl, xc, xr, nz,
):
    weight_copy = pltpu.make_async_copy(w_hbm.at[k], w_ref, sem)
    weight_copy.start()
    noise_copy = pltpu.make_async_copy(noise_hbm.at[j], noise_raw, noise_sem)
    noise_copy.start()
    noise_copy.wait()
    noise_wide[...] = noise_raw[...].astype(jnp.float32)
    noise = noise_wide[pl.ds(cut, m), pl.ds(cut * cols, n * cols), :]
    channels = w_ref.shape[-1]
    rows_in = m * n * cols
    rows_out = (m - 2) * (n - 2) * cols
    width = (m - num_frames) // 2
    level = lv_ref[k]
    noise = noise.reshape(m * n * cols, w_ref.shape[-1])
    noisy = prior_ref[...].astype(jnp.float32) + level * noise
    mean_sq = jnp.mean(noisy * noisy, axis=-1, keepdims=True)
    normalized = (noisy * lax.rsqrt(mean_sq + 1e-05)).astype(jnp.bfloat16).astype(jnp.float32)
    shape4 = (m, n, cols, channels)
    frame_at = offs_ref[0] - width + lax.broadcasted_iota(jnp.int32, shape4, 0)
    row_at = offs_ref[1] - width + lax.broadcasted_iota(jnp.int32, shape4, 1)
    inside = (frame_at >= 0) & (frame_at < total_frames) & (row_at >= 0) & (row_at < total_rows)
    inside = inside.reshape(m, n * cols, channels)
    normalized = jnp.where(inside, normalized.reshape(m, n * cols, channels), 0.0)
    normalized = normalized.reshape(rows_in, channels)
    col = lax.broadcasted_iota(jnp.int32, (rows_in, channels), 0) % cols
    left = jnp.where(col == 0, 0.0, pltpu.roll(normalized, 1, 0))
    right = jnp.where(col == cols - 1, 0.0, pltpu.roll(normalized, rows_in - 1, 0))
    xl[...] = left.reshape(m, n * cols, channels)
    xc[...] = normalized.reshape(m, n * cols, channels)
    xr[...] = right.reshape(m, n * cols, channels)
    nz[...] = noisy.reshape(m, n * cols, channels)
    weight_copy.wait()
    views = (xl, xc, xr)
    acc = jnp.zeros((rows_out, channels), jnp.float32)
    for tap in range(9):
        a, b = tap // 3, tap % 3
        v = views[b][pl.ds(1, m - 2), pl.ds(a * cols, (n - 2) * cols), :]
        v = v.reshape(rows_out, channels).astype(jnp.bfloat16)
        acc = acc + jnp.dot(v, w_ref[tap], preferred_element_type=jnp.float32)
    for t in range(3):
        v = xc[pl.ds(t, m - 2), pl.ds(cols, (n - 2) * cols), :]
        v = v.reshape(rows_out, channels).astype(jnp.bfloat16)
        acc = acc + jnp.dot(v, w_ref[9 + t], preferred_element_type=jnp.float32)
    act = (acc / (1.0 + jnp.exp(-acc))).astype(jnp.bfloat16)
    est = jnp.dot(act, w_ref[12], preferred_element_type=jnp.float32)
    center = nz[pl.ds(1, m - 2), pl.ds(cols, (n - 2) * cols), :].reshape(rows_out, channels)
    result = center - level * est
    out_ref[...] = result.astype(out_ref.dtype)
    nz[pl.ds(0, m - 2), pl.ds(0, (n - 2) * cols), :] = result.reshape(m - 2, (n - 2) * cols, channels)
    crop = nz[pl.ds(inner, num_frames), pl.ds(inner * cols, num_rows * cols), :]
    crop_ref[...] = crop.reshape(num_frames * num_rows * cols, channels).astype(crop_ref.dtype)


def section_call(offs, levels, prior, noise, packed, k, j, m, n, cols, num_frames, num_rows, totals):
    channels = packed.shape[-1]
    rows_in = m * n * cols
    rows_out = (m - 2) * (n - 2) * cols
    rows_crop = num_frames * num_rows * cols
    inner = (m - 2 - num_frames) // 2
    flops = 2 * rows_out * channels * channels * 13
    nbytes = 2 * 2 * rows_in * channels + 2 * 13 * channels * channels
    nbytes += 2 * (rows_out + rows_crop) * channels
    scratch = pltpu.VMEM((m, n * cols, channels), jnp.float32)
    smem = pl.BlockSpec(memory_space=pltpu.SMEM)
    vmem = pl.BlockSpec(memory_space=pltpu.VMEM)
    return pl.pallas_call(
        functools.partial(
            section_kernel, m, n, cols, inner, num_frames, num_rows, totals[0], totals[1], k, j,
            (noise.shape[1] - m) // 2,
        ),
        out_shape=(
            jax.ShapeDtypeStruct((rows_out, channels), jnp.bfloat16),
            jax.ShapeDtypeStruct((rows_crop, channels), jnp.bfloat16),
        ),
        in_specs=[smem, smem, vmem, pl.BlockSpec(memory_space=pl.ANY), pl.BlockSpec(memory_space=pl.ANY)],
        out_specs=(vmem, vmem),
        scratch_shapes=[
            pltpu.VMEM(packed.shape[1:], packed.dtype),
            pltpu.SemaphoreType.DMA(()),
            pltpu.VMEM(noise.shape[1:], noise.dtype),
            pltpu.SemaphoreType.DMA(()),
            pltpu.VMEM(noise.shape[1:], jnp.float32),
        ]
        + [scratch] * 4,
        cost_estimate=pl.CostEstimate(
            flops=flops, bytes_accessed=nbytes, transcendentals=rows_out * channels
        ),
    )(offs, levels, prior, noise, packed)


def extend(block, width, frame_dim, row_dim):
    for axis, dim in (("frames", frame_dim), ("space", row_dim)):
        count = lax.axis_size(axis)
        forward = [(i, i + 1) for i in range(count - 1)]
        backward = [(i + 1, i) for i in range(count - 1)]
        size = block.shape[dim]
        low = lax.ppermute(lax.slice_in_dim(block, size - width, size, axis=dim), axis, forward)
        high = lax.ppermute(lax.slice_in_dim(block, 0, width, axis=dim), axis, backward)
        block = jnp.concatenate([low, block, high], axis=dim)
    return block


def denoise(offs, levels, previous, noise_round, j, packed, k, num_frames, num_rows, totals):
    num_videos, m, n, num_cols, channels = previous.shape
    outs = []
    crops = []
    for v in range(num_videos):
        out, crop = section_call(
            offs,
            levels,
            previous[v].reshape(-1, channels),
            noise_round,
            packed,
            k,
            j,
            m,
            n,
            num_cols,
            num_frames,
            num_rows,
            totals,
        )
        outs.append(out.reshape(m - 2, n - 2, num_cols, channels))
        crops.append(crop)
    return jnp.stack(outs), jnp.stack(crops)


def flat_noise(noise):
    groups, _, big_m, big_n, cols, channels = noise.shape
    return noise.reshape(groups, big_m, big_n * cols, channels)


def on_device(
    base_frames, section_noise, noise_levels, spatial_kernel, temporal_kernel, output_weight
):
    place = lax.axis_index("section")
    sections = lax.axis_size("section")
    video_count, num_frames, num_rows = base_frames.shape[:3]
    per_device = video_count // sections
    halo = HALO
    noise_t = lax.all_to_all(section_noise[0], "section", 0, 0, tiled=True)
    noise_t = noise_t.reshape((sections, per_device) + noise_t.shape[1:])
    channels = spatial_kernel.shape[-1]
    level_slab = jnp.broadcast_to(
        noise_levels.reshape(1, 1, 1, 1), (1, 1, channels, channels)
    ).astype(spatial_kernel.dtype)
    packed = jnp.concatenate(
        [spatial_kernel, temporal_kernel, output_weight[:, None], level_slab], axis=1
    )
    packed = lax.all_gather(packed, "section", tiled=True)
    incoming = lax.dynamic_slice_in_dim(base_frames, place * per_device, per_device, 0)
    levels = packed[:, 13, 0, 0].astype(jnp.float32)
    offs = jnp.stack(
        [lax.axis_index("frames") * num_frames, lax.axis_index("space") * num_rows]
    ).astype(jnp.int32)
    totals = (num_frames * lax.axis_size("frames"), num_rows * lax.axis_size("space"))
    both = extend(jnp.concatenate([incoming[None], noise_t[:halo]], axis=0), halo, 2, 3)
    prior_ext = both[0]
    noise_round = flat_noise(both[1:])
    results = []
    for k in range(sections):
        j = k % halo
        if j == 0 and k > 0:
            prior_ext = extend(prior_ext, halo, 1, 2)
            noise_round = noise_next
        width = halo - j
        cut = halo - width
        prior_ext, crop = denoise(
            offs, levels, prior_ext, noise_round, j, packed, k, num_frames, num_rows, totals
        )
        results.append(crop)
        if j == 0 and k + halo < sections:
            later, _ = lax.optimization_barrier((noise_t[k + halo : k + 2 * halo], crop))
            noise_next = flat_noise(extend(later, halo, 2, 3))
    num_cols, channels = base_frames.shape[3:]
    stacked = jnp.stack(results).reshape(
        (sections, per_device, num_frames, num_rows, num_cols, channels)
    )
    return lax.all_to_all(stacked, "section", 0, 1, tiled=True)


def solution(mesh):
    return jax.shard_map(
        on_device,
        mesh=mesh,
        in_specs=(
            P(None, "frames", "space", None, None),
            P("section", None, "frames", "space", None, None),
            P("section"),
            P("section", None, None, None),
            P("section", None, None, None),
            P("section", None, None),
        ),
        out_specs=P("section", None, "frames", "space", None, None),
        check_vma=False,
    )
```

```python
import jax
import jax.numpy as jnp
from jax import lax
import functools
from jax.experimental import pallas as pl
from jax.experimental.pallas import tpu as pltpu
from jax.sharding import PartitionSpec as P

HALO = 4


def section_kernel(
    m, n, cols, inner, num_frames, num_rows, total_frames, total_rows, k,
    offs_ref, lv_ref, prior_ref, noise_ref, w_hbm, stack_in, out_ref, stack_ref,
    w_ref, sem, crop_buf, crop_sem, xl, xc, xr, nz,
):
    weight_copy = pltpu.make_async_copy(w_hbm.at[k], w_ref, sem)
    weight_copy.start()
    channels = w_ref.shape[-1]
    rows_in = m * n * cols
    rows_out = (m - 2) * (n - 2) * cols
    width = (m - num_frames) // 2
    level = lv_ref[k]
    noisy = prior_ref[...].astype(jnp.float32) + level * noise_ref[...].astype(jnp.float32)
    mean_sq = jnp.mean(noisy * noisy, axis=-1, keepdims=True)
    normalized = (noisy * lax.rsqrt(mean_sq + 1e-05)).astype(jnp.bfloat16).astype(jnp.float32)
    shape4 = (m, n, cols, channels)
    frame_at = offs_ref[0] - width + lax.broadcasted_iota(jnp.int32, shape4, 0)
    row_at = offs_ref[1] - width + lax.broadcasted_iota(jnp.int32, shape4, 1)
    inside = (frame_at >= 0) & (frame_at < total_frames) & (row_at >= 0) & (row_at < total_rows)
    inside = inside.reshape(m, n * cols, channels)
    normalized = jnp.where(inside, normalized.reshape(m, n * cols, channels), 0.0)
    normalized = normalized.reshape(rows_in, channels)
    col = lax.broadcasted_iota(jnp.int32, (rows_in, channels), 0) % cols
    left = jnp.where(col == 0, 0.0, pltpu.roll(normalized, 1, 0))
    right = jnp.where(col == cols - 1, 0.0, pltpu.roll(normalized, rows_in - 1, 0))
    xl[...] = left.reshape(m, n * cols, channels)
    xc[...] = normalized.reshape(m, n * cols, channels)
    xr[...] = right.reshape(m, n * cols, channels)
    nz[...] = noisy.reshape(m, n * cols, channels)
    weight_copy.wait()
    views = (xl, xc, xr)
    acc = jnp.zeros((rows_out, channels), jnp.float32)
    for tap in range(9):
        a, b = tap // 3, tap % 3
        v = views[b][pl.ds(1, m - 2), pl.ds(a * cols, (n - 2) * cols), :]
        v = v.reshape(rows_out, channels).astype(jnp.bfloat16)
        acc = acc + jnp.dot(v, w_ref[tap], preferred_element_type=jnp.float32)
    for t in range(3):
        v = xc[pl.ds(t, m - 2), pl.ds(cols, (n - 2) * cols), :]
        v = v.reshape(rows_out, channels).astype(jnp.bfloat16)
        acc = acc + jnp.dot(v, w_ref[9 + t], preferred_element_type=jnp.float32)
    act = (acc / (1.0 + jnp.exp(-acc))).astype(jnp.bfloat16)
    est = jnp.dot(act, w_ref[12], preferred_element_type=jnp.float32)
    center = nz[pl.ds(1, m - 2), pl.ds(cols, (n - 2) * cols), :].reshape(rows_out, channels)
    result = center - level * est
    out_ref[...] = result.astype(out_ref.dtype)
    nz[pl.ds(0, m - 2), pl.ds(0, (n - 2) * cols), :] = result.reshape(m - 2, (n - 2) * cols, channels)
    crop = nz[pl.ds(inner, num_frames), pl.ds(inner * cols, num_rows * cols), :]
    crop_buf[...] = crop.reshape(num_frames * num_rows * cols, channels).astype(crop_buf.dtype)
    crop_copy = pltpu.make_async_copy(crop_buf, stack_ref.at[k], crop_sem)
    crop_copy.start()
    crop_copy.wait()


def section_call(offs, levels, prior, noise, packed, stack, k, m, n, cols, num_frames, num_rows, totals):
    channels = packed.shape[-1]
    rows_in = m * n * cols
    rows_out = (m - 2) * (n - 2) * cols
    rows_crop = num_frames * num_rows * cols
    inner = (m - 2 - num_frames) // 2
    flops = 2 * rows_out * channels * channels * 13
    nbytes = 2 * 2 * rows_in * channels + 2 * 13 * channels * channels
    nbytes += 2 * (rows_out + rows_crop) * channels
    scratch = pltpu.VMEM((m, n * cols, channels), jnp.float32)
    smem = pl.BlockSpec(memory_space=pltpu.SMEM)
    vmem = pl.BlockSpec(memory_space=pltpu.VMEM)
    return pl.pallas_call(
        functools.partial(
            section_kernel, m, n, cols, inner, num_frames, num_rows, totals[0], totals[1], k
        ),
        out_shape=(
            jax.ShapeDtypeStruct((rows_out, channels), jnp.bfloat16),
            jax.ShapeDtypeStruct(stack.shape, stack.dtype),
        ),
        in_specs=[smem, smem, vmem, vmem, pl.BlockSpec(memory_space=pl.ANY)] * 1
        + [pl.BlockSpec(memory_space=pl.ANY)],
        out_specs=(vmem, pl.BlockSpec(memory_space=pl.ANY)),
        input_output_aliases={5: 1},
        scratch_shapes=[
            pltpu.VMEM(packed.shape[1:], packed.dtype),
            pltpu.SemaphoreType.DMA(()),
            pltpu.VMEM((rows_crop, channels), jnp.bfloat16),
            pltpu.SemaphoreType.DMA(()),
        ]
        + [scratch] * 4,
        cost_estimate=pl.CostEstimate(
            flops=flops, bytes_accessed=nbytes, transcendentals=rows_out * channels
        ),
    )(offs, levels, prior, noise, packed, stack)


def extend(block, width, frame_dim, row_dim):
    for axis, dim in (("frames", frame_dim), ("space", row_dim)):
        count = lax.axis_size(axis)
        forward = [(i, i + 1) for i in range(count - 1)]
        backward = [(i + 1, i) for i in range(count - 1)]
        size = block.shape[dim]
        low = lax.ppermute(lax.slice_in_dim(block, size - width, size, axis=dim), axis, forward)
        high = lax.ppermute(lax.slice_in_dim(block, 0, width, axis=dim), axis, backward)
        block = jnp.concatenate([low, block, high], axis=dim)
    return block


def denoise(offs, levels, previous, noise_part, packed, stack, k, num_frames, num_rows, totals):
    num_videos, m, n, num_cols, channels = previous.shape
    outs = []
    for v in range(num_videos):
        out, stack = section_call(
            offs,
            levels,
            previous[v].reshape(-1, channels),
            noise_part[v].reshape(-1, channels),
            packed,
            stack,
            k,
            m,
            n,
            num_cols,
            num_frames,
            num_rows,
            totals,
        )
        outs.append(out.reshape(m - 2, n - 2, num_cols, channels))
    return jnp.stack(outs), stack


def on_device(
    base_frames, section_noise, noise_levels, spatial_kernel, temporal_kernel, output_weight
):
    place = lax.axis_index("section")
    sections = lax.axis_size("section")
    video_count, num_frames, num_rows = base_frames.shape[:3]
    per_device = video_count // sections
    halo = HALO
    noise_t = lax.all_to_all(section_noise[0], "section", 0, 0, tiled=True)
    noise_t = noise_t.reshape((sections, per_device) + noise_t.shape[1:])
    channels = spatial_kernel.shape[-1]
    level_slab = jnp.broadcast_to(
        noise_levels.reshape(1, 1, 1, 1), (1, 1, channels, channels)
    ).astype(spatial_kernel.dtype)
    packed = jnp.concatenate(
        [spatial_kernel, temporal_kernel, output_weight[:, None], level_slab], axis=1
    )
    packed = lax.all_gather(packed, "section", tiled=True)
    incoming = lax.dynamic_slice_in_dim(base_frames, place * per_device, per_device, 0)
    levels = packed[:, 13, 0, 0].astype(jnp.float32)
    offs = jnp.stack(
        [lax.axis_index("frames") * num_frames, lax.axis_index("space") * num_rows]
    ).astype(jnp.int32)
    totals = (num_frames * lax.axis_size("frames"), num_rows * lax.axis_size("space"))
    both = extend(jnp.concatenate([incoming[None], noise_t[:halo]], axis=0), halo, 2, 3)
    prior_ext = both[0]
    noise_round = both[1:]
    num_cols, channels = base_frames.shape[3:]
    stack = jnp.zeros((sections, num_frames * num_rows * num_cols, channels), jnp.bfloat16)
    for k in range(sections):
        j = k % halo
        if j == 0 and k > 0:
            prior_ext = extend(prior_ext, halo, 1, 2)
            noise_round = noise_next
        width = halo - j
        cut = halo - width
        noise_here = noise_round[
            j, :, cut : cut + num_frames + 2 * width, cut : cut + num_rows + 2 * width
        ]
        prior_ext, stack = denoise(
            offs, levels, prior_ext, noise_here, packed, stack, k, num_frames, num_rows, totals
        )
        if j == 0 and k + halo < sections:
            noise_next = extend(noise_t[k + halo : k + 2 * halo], halo, 2, 3)
    stacked = stack.reshape(
        (sections, per_device, num_frames, num_rows, num_cols, channels)
    )
    return lax.all_to_all(stacked, "section", 0, 1, tiled=True)


def solution(mesh):
    return jax.shard_map(
        on_device,
        mesh=mesh,
        in_specs=(
            P(None, "frames", "space", None, None),
            P("section", None, "frames", "space", None, None),
            P("section"),
            P("section", None, None, None),
            P("section", None, None, None),
            P("section", None, None),
        ),
        out_specs=P("section", None, "frames", "space", None, None),
        check_vma=False,
    )
```

```python
import jax
import jax.numpy as jnp
from jax import lax
import functools
from jax.experimental import pallas as pl
from jax.experimental.pallas import tpu as pltpu
from jax.sharding import PartitionSpec as P

HALO = 4


def section_kernel(
    m, n, cols, inner, num_frames, num_rows, total_frames, total_rows, k,
    offs_ref, lv_ref, prior_ref, noise_ref, w_hbm, out_ref, crop_ref, w_ref, sem, xl, xc, xr, nz,
):
    weight_copy = pltpu.make_async_copy(w_hbm.at[k], w_ref, sem)
    weight_copy.start()
    channels = w_ref.shape[-1]
    rows_in = m * n * cols
    rows_out = (m - 2) * (n - 2) * cols
    width = (m - num_frames) // 2
    level = lv_ref[k]
    noisy = prior_ref[...].astype(jnp.float32) + level * noise_ref[...].astype(jnp.float32)
    mean_sq = jnp.mean(noisy * noisy, axis=-1, keepdims=True)
    normalized = (noisy * lax.rsqrt(mean_sq + 1e-05)).astype(jnp.bfloat16).astype(jnp.float32)
    shape4 = (m, n, cols, channels)
    frame_at = offs_ref[0] - width + lax.broadcasted_iota(jnp.int32, shape4, 0)
    row_at = offs_ref[1] - width + lax.broadcasted_iota(jnp.int32, shape4, 1)
    inside = (frame_at >= 0) & (frame_at < total_frames) & (row_at >= 0) & (row_at < total_rows)
    inside = inside.reshape(m, n * cols, channels)
    normalized = jnp.where(inside, normalized.reshape(m, n * cols, channels), 0.0)
    normalized = normalized.reshape(rows_in, channels)
    col = lax.broadcasted_iota(jnp.int32, (rows_in, channels), 0) % cols
    left = jnp.where(col == 0, 0.0, pltpu.roll(normalized, 1, 0))
    right = jnp.where(col == cols - 1, 0.0, pltpu.roll(normalized, rows_in - 1, 0))
    xl[...] = left.reshape(m, n * cols, channels)
    xc[...] = normalized.reshape(m, n * cols, channels)
    xr[...] = right.reshape(m, n * cols, channels)
    nz[...] = noisy.reshape(m, n * cols, channels)
    weight_copy.wait()
    views = (xl, xc, xr)
    acc = jnp.zeros((rows_out, channels), jnp.float32)
    for tap in range(9):
        a, b = tap // 3, tap % 3
        v = views[b][pl.ds(1, m - 2), pl.ds(a * cols, (n - 2) * cols), :]
        v = v.reshape(rows_out, channels).astype(jnp.bfloat16)
        acc = acc + jnp.dot(v, w_ref[tap], preferred_element_type=jnp.float32)
    for t in range(3):
        v = xc[pl.ds(t, m - 2), pl.ds(cols, (n - 2) * cols), :]
        v = v.reshape(rows_out, channels).astype(jnp.bfloat16)
        acc = acc + jnp.dot(v, w_ref[9 + t], preferred_element_type=jnp.float32)
    act = (acc / (1.0 + jnp.exp(-acc))).astype(jnp.bfloat16)
    est = jnp.dot(act, w_ref[12], preferred_element_type=jnp.float32)
    center = nz[pl.ds(1, m - 2), pl.ds(cols, (n - 2) * cols), :].reshape(rows_out, channels)
    result = center - level * est
    out_ref[...] = result.astype(out_ref.dtype)
    nz[pl.ds(0, m - 2), pl.ds(0, (n - 2) * cols), :] = result.reshape(m - 2, (n - 2) * cols, channels)
    crop = nz[pl.ds(inner, num_frames), pl.ds(inner * cols, num_rows * cols), :]
    crop_ref[...] = crop.reshape(num_frames * num_rows * cols, channels).astype(crop_ref.dtype)


def section_call(offs, levels, prior, noise, packed, k, m, n, cols, num_frames, num_rows, totals):
    channels = packed.shape[-1]
    rows_in = m * n * cols
    rows_out = (m - 2) * (n - 2) * cols
    rows_crop = num_frames * num_rows * cols
    inner = (m - 2 - num_frames) // 2
    flops = 2 * rows_out * channels * channels * 13
    nbytes = 2 * 2 * rows_in * channels + 2 * 13 * channels * channels
    nbytes += 2 * (rows_out + rows_crop) * channels
    scratch = pltpu.VMEM((m, n * cols, channels), jnp.float32)
    smem = pl.BlockSpec(memory_space=pltpu.SMEM)
    vmem = pl.BlockSpec(memory_space=pltpu.VMEM)
    return pl.pallas_call(
        functools.partial(
            section_kernel, m, n, cols, inner, num_frames, num_rows, totals[0], totals[1], k
        ),
        out_shape=(
            jax.ShapeDtypeStruct((rows_out, channels), jnp.bfloat16),
            jax.ShapeDtypeStruct((rows_crop, channels), jnp.bfloat16),
        ),
        in_specs=[smem, smem, vmem, vmem, pl.BlockSpec(memory_space=pl.ANY)],
        out_specs=(vmem, vmem),
        scratch_shapes=[
            pltpu.VMEM(packed.shape[1:], packed.dtype),
            pltpu.SemaphoreType.DMA(()),
        ]
        + [scratch] * 4,
        cost_estimate=pl.CostEstimate(
            flops=flops, bytes_accessed=nbytes, transcendentals=rows_out * channels
        ),
    )(offs, levels, prior, noise, packed)


def extend(block, width, frame_dim, row_dim):
    for axis, dim in (("frames", frame_dim), ("space", row_dim)):
        count = lax.axis_size(axis)
        forward = [(i, i + 1) for i in range(count - 1)]
        backward = [(i + 1, i) for i in range(count - 1)]
        size = block.shape[dim]
        low = lax.ppermute(lax.slice_in_dim(block, size - width, size, axis=dim), axis, forward)
        high = lax.ppermute(lax.slice_in_dim(block, 0, width, axis=dim), axis, backward)
        block = jnp.concatenate([low, block, high], axis=dim)
    return block


def denoise(offs, levels, previous, noise_part, packed, k, num_frames, num_rows, totals):
    num_videos, m, n, num_cols, channels = previous.shape
    outs = []
    crops = []
    for v in range(num_videos):
        out, crop = section_call(
            offs,
            levels,
            previous[v].reshape(-1, channels),
            noise_part[v].reshape(-1, channels),
            packed,
            k,
            m,
            n,
            num_cols,
            num_frames,
            num_rows,
            totals,
        )
        outs.append(out.reshape(m - 2, n - 2, num_cols, channels))
        crops.append(crop)
    return jnp.stack(outs), jnp.stack(crops)


def on_device(
    base_frames, section_noise, noise_levels, spatial_kernel, temporal_kernel, output_weight
):
    place = lax.axis_index("section")
    sections = lax.axis_size("section")
    video_count, num_frames, num_rows = base_frames.shape[:3]
    per_device = video_count // sections
    halo = HALO
    noise_t = lax.all_to_all(section_noise[0], "section", 0, 0, tiled=True)
    noise_t = noise_t.reshape((sections, per_device) + noise_t.shape[1:])
    channels = spatial_kernel.shape[-1]
    level_slab = jnp.broadcast_to(
        noise_levels.reshape(1, 1, 1, 1), (1, 1, channels, channels)
    ).astype(spatial_kernel.dtype)
    packed = jnp.concatenate(
        [spatial_kernel, temporal_kernel, output_weight[:, None], level_slab], axis=1
    )
    packed = lax.all_gather(packed, "section", tiled=True)
    incoming = lax.dynamic_slice_in_dim(base_frames, place * per_device, per_device, 0)
    levels = packed[:, 13, 0, 0].astype(jnp.float32)
    offs = jnp.stack(
        [lax.axis_index("frames") * num_frames, lax.axis_index("space") * num_rows]
    ).astype(jnp.int32)
    totals = (num_frames * lax.axis_size("frames"), num_rows * lax.axis_size("space"))
    both = extend(jnp.concatenate([incoming[None], noise_t[:halo]], axis=0), halo, 2, 3)
    prior_ext = both[0]
    noise_round = both[1:]
    results = []
    for k in range(sections):
        j = k % halo
        if j == 0 and k > 0:
            noise_round, prior_ext = lax.optimization_barrier((noise_next, prior_ext))
            prior_ext = extend(prior_ext, halo, 1, 2)
        width = halo - j
        cut = halo - width
        noise_here = noise_round[
            j, :, cut : cut + num_frames + 2 * width, cut : cut + num_rows + 2 * width
        ]
        prior_ext, crop = denoise(
            offs, levels, prior_ext, noise_here, packed, k, num_frames, num_rows, totals
        )
        results.append(crop)
        if j == 0 and k + halo < sections:
            later, _ = lax.optimization_barrier((noise_t[k + halo : k + 2 * halo], crop))
            noise_next = extend(later, halo, 2, 3)
    num_cols, channels = base_frames.shape[3:]
    stacked = jnp.stack(results).reshape(
        (sections, per_device, num_frames, num_rows, num_cols, channels)
    )
    return lax.all_to_all(stacked, "section", 0, 1, tiled=True)


def solution(mesh):
    return jax.shard_map(
        on_device,
        mesh=mesh,
        in_specs=(
            P(None, "frames", "space", None, None),
            P("section", None, "frames", "space", None, None),
            P("section"),
            P("section", None, None, None),
            P("section", None, None, None),
            P("section", None, None),
        ),
        out_specs=P("section", None, "frames", "space", None, None),
        check_vma=False,
    )
```

```python
import jax
import jax.numpy as jnp
from jax import lax
import functools
from jax.experimental import pallas as pl
from jax.experimental.pallas import tpu as pltpu
from jax.sharding import PartitionSpec as P

HALO = 4


def section_kernel(
    m, n, cols, inner, num_frames, num_rows, total_frames, total_rows, k,
    offs_ref, prior_ref, noise_ref, w_hbm, out_ref, crop_ref, w_ref, sem, xl, xc, xr, nz,
):
    weight_copy = pltpu.make_async_copy(w_hbm.at[k], w_ref, sem)
    weight_copy.start()
    channels = w_ref.shape[-1]
    rows_in = m * n * cols
    rows_out = (m - 2) * (n - 2) * cols
    width = (m - num_frames) // 2
    prior = prior_ref[...].astype(jnp.float32)
    noise = noise_ref[...].astype(jnp.float32)
    weight_copy.wait()
    level = w_ref[13][0:1, :].astype(jnp.float32)
    noisy = prior + level * noise
    mean_sq = jnp.mean(noisy * noisy, axis=-1, keepdims=True)
    normalized = (noisy * lax.rsqrt(mean_sq + 1e-05)).astype(jnp.bfloat16).astype(jnp.float32)
    shape4 = (m, n, cols, channels)
    frame_at = offs_ref[0] - width + lax.broadcasted_iota(jnp.int32, shape4, 0)
    row_at = offs_ref[1] - width + lax.broadcasted_iota(jnp.int32, shape4, 1)
    inside = (frame_at >= 0) & (frame_at < total_frames) & (row_at >= 0) & (row_at < total_rows)
    inside = inside.reshape(m, n * cols, channels)
    normalized = jnp.where(inside, normalized.reshape(m, n * cols, channels), 0.0)
    normalized = normalized.reshape(rows_in, channels)
    col = lax.broadcasted_iota(jnp.int32, (rows_in, channels), 0) % cols
    left = jnp.where(col == 0, 0.0, pltpu.roll(normalized, 1, 0))
    right = jnp.where(col == cols - 1, 0.0, pltpu.roll(normalized, rows_in - 1, 0))
    xl[...] = left.reshape(m, n * cols, channels)
    xc[...] = normalized.reshape(m, n * cols, channels)
    xr[...] = right.reshape(m, n * cols, channels)
    nz[...] = noisy.reshape(m, n * cols, channels)
    views = (xl, xc, xr)
    acc = jnp.zeros((rows_out, channels), jnp.float32)
    for tap in range(9):
        a, b = tap // 3, tap % 3
        v = views[b][pl.ds(1, m - 2), pl.ds(a * cols, (n - 2) * cols), :]
        v = v.reshape(rows_out, channels).astype(jnp.bfloat16)
        acc = acc + jnp.dot(v, w_ref[tap], preferred_element_type=jnp.float32)
    for t in range(3):
        v = xc[pl.ds(t, m - 2), pl.ds(cols, (n - 2) * cols), :]
        v = v.reshape(rows_out, channels).astype(jnp.bfloat16)
        acc = acc + jnp.dot(v, w_ref[9 + t], preferred_element_type=jnp.float32)
    act = (acc / (1.0 + jnp.exp(-acc))).astype(jnp.bfloat16)
    est = jnp.dot(act, w_ref[12], preferred_element_type=jnp.float32)
    center = nz[pl.ds(1, m - 2), pl.ds(cols, (n - 2) * cols), :].reshape(rows_out, channels)
    result = center - level * est
    out_ref[...] = result.astype(out_ref.dtype)
    nz[pl.ds(0, m - 2), pl.ds(0, (n - 2) * cols), :] = result.reshape(m - 2, (n - 2) * cols, channels)
    crop = nz[pl.ds(inner, num_frames), pl.ds(inner * cols, num_rows * cols), :]
    crop_ref[...] = crop.reshape(num_frames * num_rows * cols, channels).astype(crop_ref.dtype)


def section_call(offs, prior, noise, packed, k, m, n, cols, num_frames, num_rows, totals):
    channels = packed.shape[-1]
    rows_in = m * n * cols
    rows_out = (m - 2) * (n - 2) * cols
    rows_crop = num_frames * num_rows * cols
    inner = (m - 2 - num_frames) // 2
    flops = 2 * rows_out * channels * channels * 13
    nbytes = 2 * 2 * rows_in * channels + 2 * 13 * channels * channels
    nbytes += 2 * (rows_out + rows_crop) * channels
    scratch = pltpu.VMEM((m, n * cols, channels), jnp.float32)
    smem = pl.BlockSpec(memory_space=pltpu.SMEM)
    vmem = pl.BlockSpec(memory_space=pltpu.VMEM)
    return pl.pallas_call(
        functools.partial(
            section_kernel, m, n, cols, inner, num_frames, num_rows, totals[0], totals[1], k
        ),
        out_shape=(
            jax.ShapeDtypeStruct((rows_out, channels), jnp.bfloat16),
            jax.ShapeDtypeStruct((rows_crop, channels), jnp.bfloat16),
        ),
        in_specs=[smem, vmem, vmem, pl.BlockSpec(memory_space=pl.ANY)],
        out_specs=(vmem, vmem),
        scratch_shapes=[
            pltpu.VMEM(packed.shape[1:], packed.dtype),
            pltpu.SemaphoreType.DMA(()),
        ]
        + [scratch] * 4,
        cost_estimate=pl.CostEstimate(
            flops=flops, bytes_accessed=nbytes, transcendentals=rows_out * channels
        ),
    )(offs, prior, noise, packed)


def extend(block, width, frame_dim, row_dim):
    for axis, dim in (("frames", frame_dim), ("space", row_dim)):
        count = lax.axis_size(axis)
        forward = [(i, i + 1) for i in range(count - 1)]
        backward = [(i + 1, i) for i in range(count - 1)]
        size = block.shape[dim]
        low = lax.ppermute(lax.slice_in_dim(block, size - width, size, axis=dim), axis, forward)
        high = lax.ppermute(lax.slice_in_dim(block, 0, width, axis=dim), axis, backward)
        block = jnp.concatenate([low, block, high], axis=dim)
    return block


def denoise(offs, previous, noise_part, packed, k, num_frames, num_rows, totals):
    num_videos, m, n, num_cols, channels = previous.shape
    outs = []
    crops = []
    for v in range(num_videos):
        out, crop = section_call(
            offs,
            previous[v].reshape(-1, channels),
            noise_part[v].reshape(-1, channels),
            packed,
            k,
            m,
            n,
            num_cols,
            num_frames,
            num_rows,
            totals,
        )
        outs.append(out.reshape(m - 2, n - 2, num_cols, channels))
        crops.append(crop)
    return jnp.stack(outs), jnp.stack(crops)


def on_device(
    base_frames, section_noise, noise_levels, spatial_kernel, temporal_kernel, output_weight
):
    place = lax.axis_index("section")
    sections = lax.axis_size("section")
    video_count, num_frames, num_rows = base_frames.shape[:3]
    per_device = video_count // sections
    halo = HALO
    noise_t = lax.all_to_all(section_noise[0], "section", 0, 0, tiled=True)
    noise_t = noise_t.reshape((sections, per_device) + noise_t.shape[1:])
    channels = spatial_kernel.shape[-1]
    level_slab = jnp.broadcast_to(
        noise_levels.reshape(1, 1, 1, 1), (1, 1, channels, channels)
    ).astype(spatial_kernel.dtype)
    packed = jnp.concatenate(
        [spatial_kernel, temporal_kernel, output_weight[:, None], level_slab], axis=1
    )
    packed = lax.all_gather(packed, "section", tiled=True)
    incoming = lax.dynamic_slice_in_dim(base_frames, place * per_device, per_device, 0)
    offs = jnp.stack(
        [lax.axis_index("frames") * num_frames, lax.axis_index("space") * num_rows]
    ).astype(jnp.int32)
    totals = (num_frames * lax.axis_size("frames"), num_rows * lax.axis_size("space"))
    both = extend(jnp.concatenate([incoming[None], noise_t[:halo]], axis=0), halo, 2, 3)
    prior_ext = both[0]
    noise_round = both[1:]
    results = []
    for k in range(sections):
        j = k % halo
        if j == 0 and k > 0:
            prior_ext = extend(prior_ext, halo, 1, 2)
            noise_round = noise_next
        width = halo - j
        cut = halo - width
        noise_here = noise_round[
            j, :, cut : cut + num_frames + 2 * width, cut : cut + num_rows + 2 * width
        ]
        prior_ext, crop = denoise(
            offs, prior_ext, noise_here, packed, k, num_frames, num_rows, totals
        )
        results.append(crop)
        if j == 0 and k + halo < sections:
            later, _ = lax.optimization_barrier((noise_t[k + halo : k + 2 * halo], crop))
            noise_next = extend(later, halo, 2, 3)
    num_cols, channels = base_frames.shape[3:]
    stacked = jnp.stack(results).reshape(
        (sections, per_device, num_frames, num_rows, num_cols, channels)
    )
    return lax.all_to_all(stacked, "section", 0, 1, tiled=True)


def solution(mesh):
    return jax.shard_map(
        on_device,
        mesh=mesh,
        in_specs=(
            P(None, "frames", "space", None, None),
            P("section", None, "frames", "space", None, None),
            P("section"),
            P("section", None, None, None),
            P("section", None, None, None),
            P("section", None, None),
        ),
        out_specs=P("section", None, "frames", "space", None, None),
        check_vma=False,
    )
```

```python
import jax
import jax.numpy as jnp
from jax import lax
import functools
from jax.experimental import pallas as pl
from jax.experimental.pallas import tpu as pltpu
from jax.sharding import PartitionSpec as P

HALO = 4


def section_kernel(
    m, n, cols, inner, num_frames, num_rows, total_frames, total_rows, k,
    offs_ref, lv_ref, prior_ref, noise_ref, w_hbm, out_ref, crop_ref, w_ref, sem, xl, xc, xr, nz,
):
    weight_copy = pltpu.make_async_copy(w_hbm.at[k], w_ref, sem)
    weight_copy.start()
    channels = w_ref.shape[-1]
    rows_in = m * n * cols
    rows_out = (m - 2) * (n - 2) * cols
    width = (m - num_frames) // 2
    level = lv_ref[k]
    noisy = prior_ref[...].astype(jnp.float32) + level * noise_ref[...].astype(jnp.float32)
    mean_sq = jnp.mean(noisy * noisy, axis=-1, keepdims=True)
    normalized = (noisy * lax.rsqrt(mean_sq + 1e-05)).astype(jnp.bfloat16).astype(jnp.float32)
    shape4 = (m, n, cols, channels)
    frame_at = offs_ref[0] - width + lax.broadcasted_iota(jnp.int32, shape4, 0)
    row_at = offs_ref[1] - width + lax.broadcasted_iota(jnp.int32, shape4, 1)
    inside = (frame_at >= 0) & (frame_at < total_frames) & (row_at >= 0) & (row_at < total_rows)
    inside = inside.reshape(m, n * cols, channels)
    normalized = jnp.where(inside, normalized.reshape(m, n * cols, channels), 0.0)
    normalized = normalized.reshape(rows_in, channels)
    col = lax.broadcasted_iota(jnp.int32, (rows_in, channels), 0) % cols
    left = jnp.where(col == 0, 0.0, pltpu.roll(normalized, 1, 0))
    right = jnp.where(col == cols - 1, 0.0, pltpu.roll(normalized, rows_in - 1, 0))
    xl[...] = left.reshape(m, n * cols, channels)
    xc[...] = normalized.reshape(m, n * cols, channels)
    xr[...] = right.reshape(m, n * cols, channels)
    nz[...] = noisy.reshape(m, n * cols, channels)
    weight_copy.wait()
    views = (xl, xc, xr)
    acc = jnp.zeros((rows_out, channels), jnp.float32)
    for tap in range(9):
        a, b = tap // 3, tap % 3
        v = views[b][pl.ds(1, m - 2), pl.ds(a * cols, (n - 2) * cols), :]
        v = v.reshape(rows_out, channels).astype(jnp.bfloat16)
        acc = acc + jnp.dot(v, w_ref[tap], preferred_element_type=jnp.float32)
    for t in range(3):
        v = xc[pl.ds(t, m - 2), pl.ds(cols, (n - 2) * cols), :]
        v = v.reshape(rows_out, channels).astype(jnp.bfloat16)
        acc = acc + jnp.dot(v, w_ref[9 + t], preferred_element_type=jnp.float32)
    act = (acc / (1.0 + jnp.exp(-acc))).astype(jnp.bfloat16)
    est = jnp.dot(act, w_ref[12], preferred_element_type=jnp.float32)
    center = nz[pl.ds(1, m - 2), pl.ds(cols, (n - 2) * cols), :].reshape(rows_out, channels)
    result = center - level * est
    out_ref[...] = result.astype(out_ref.dtype)
    nz[pl.ds(0, m - 2), pl.ds(0, (n - 2) * cols), :] = result.reshape(m - 2, (n - 2) * cols, channels)
    crop = nz[pl.ds(inner, num_frames), pl.ds(inner * cols, num_rows * cols), :]
    crop_ref[...] = crop.reshape(num_frames * num_rows * cols, channels).astype(crop_ref.dtype)


def section_call(offs, levels, prior, noise, packed, k, m, n, cols, num_frames, num_rows, totals):
    channels = packed.shape[-1]
    rows_in = m * n * cols
    rows_out = (m - 2) * (n - 2) * cols
    rows_crop = num_frames * num_rows * cols
    inner = (m - 2 - num_frames) // 2
    flops = 2 * rows_out * channels * channels * 13
    nbytes = 2 * 2 * rows_in * channels + 2 * 13 * channels * channels
    nbytes += 2 * (rows_out + rows_crop) * channels
    scratch = pltpu.VMEM((m, n * cols, channels), jnp.float32)
    smem = pl.BlockSpec(memory_space=pltpu.SMEM)
    vmem = pl.BlockSpec(memory_space=pltpu.VMEM)
    return pl.pallas_call(
        functools.partial(
            section_kernel, m, n, cols, inner, num_frames, num_rows, totals[0], totals[1], k
        ),
        out_shape=(
            jax.ShapeDtypeStruct((rows_out, channels), jnp.bfloat16),
            jax.ShapeDtypeStruct((rows_crop, channels), jnp.bfloat16),
        ),
        in_specs=[smem, smem, vmem, vmem, pl.BlockSpec(memory_space=pl.ANY)],
        out_specs=(vmem, vmem),
        scratch_shapes=[
            pltpu.VMEM(packed.shape[1:], packed.dtype),
            pltpu.SemaphoreType.DMA(()),
        ]
        + [scratch] * 4,
        cost_estimate=pl.CostEstimate(
            flops=flops, bytes_accessed=nbytes, transcendentals=rows_out * channels
        ),
    )(offs, levels, prior, noise, packed)


def extend(block, width, frame_dim, row_dim):
    for axis, dim in (("frames", frame_dim), ("space", row_dim)):
        count = lax.axis_size(axis)
        forward = [(i, i + 1) for i in range(count - 1)]
        backward = [(i + 1, i) for i in range(count - 1)]
        size = block.shape[dim]
        low = lax.ppermute(lax.slice_in_dim(block, size - width, size, axis=dim), axis, forward)
        high = lax.ppermute(lax.slice_in_dim(block, 0, width, axis=dim), axis, backward)
        block = jnp.concatenate([low, block, high], axis=dim)
    return block


def denoise(offs, levels, previous, noise_part, packed, k, num_frames, num_rows, totals):
    num_videos, m, n, num_cols, channels = previous.shape
    outs = []
    crops = []
    for v in range(num_videos):
        out, crop = section_call(
            offs,
            levels,
            previous[v].reshape(-1, channels),
            noise_part[v].reshape(-1, channels),
            packed,
            k,
            m,
            n,
            num_cols,
            num_frames,
            num_rows,
            totals,
        )
        outs.append(out.reshape(m - 2, n - 2, num_cols, channels))
        crops.append(crop)
    return jnp.stack(outs), jnp.stack(crops)


def on_device(
    base_frames, section_noise, noise_levels, spatial_kernel, temporal_kernel, output_weight
):
    place = lax.axis_index("section")
    sections = lax.axis_size("section")
    video_count, num_frames, num_rows = base_frames.shape[:3]
    per_device = video_count // sections
    halo = HALO
    noise_t = lax.all_to_all(section_noise[0], "section", 0, 0, tiled=True)
    noise_t = noise_t.reshape((sections, per_device) + noise_t.shape[1:])
    channels = spatial_kernel.shape[-1]
    noise_t, spatial_kernel, temporal_kernel, output_weight, noise_levels = lax.optimization_barrier(
        (noise_t, spatial_kernel, temporal_kernel, output_weight, noise_levels)
    )
    level_slab = jnp.broadcast_to(
        noise_levels.reshape(1, 1, 1, 1), (1, 1, channels, channels)
    ).astype(spatial_kernel.dtype)
    packed = jnp.concatenate(
        [spatial_kernel, temporal_kernel, output_weight[:, None], level_slab], axis=1
    )
    packed = lax.all_gather(packed, "section", tiled=True)
    incoming = lax.dynamic_slice_in_dim(base_frames, place * per_device, per_device, 0)
    levels = packed[:, 13, 0, 0].astype(jnp.float32)
    offs = jnp.stack(
        [lax.axis_index("frames") * num_frames, lax.axis_index("space") * num_rows]
    ).astype(jnp.int32)
    totals = (num_frames * lax.axis_size("frames"), num_rows * lax.axis_size("space"))
    both = extend(jnp.concatenate([incoming[None], noise_t[:halo]], axis=0), halo, 2, 3)
    prior_ext = both[0]
    noise_round = both[1:]
    results = []
    for k in range(sections):
        j = k % halo
        if j == 0 and k > 0:
            prior_ext = extend(prior_ext, halo, 1, 2)
            noise_round = noise_next
        width = halo - j
        cut = halo - width
        noise_here = noise_round[
            j, :, cut : cut + num_frames + 2 * width, cut : cut + num_rows + 2 * width
        ]
        prior_ext, crop = denoise(
            offs, levels, prior_ext, noise_here, packed, k, num_frames, num_rows, totals
        )
        results.append(crop)
        if j == 0 and k + halo < sections:
            later, _ = lax.optimization_barrier((noise_t[k + halo : k + 2 * halo], crop))
            noise_next = extend(later, halo, 2, 3)
    num_cols, channels = base_frames.shape[3:]
    stacked = jnp.stack(results).reshape(
        (sections, per_device, num_frames, num_rows, num_cols, channels)
    )
    return lax.all_to_all(stacked, "section", 0, 1, tiled=True)


def solution(mesh):
    return jax.shard_map(
        on_device,
        mesh=mesh,
        in_specs=(
            P(None, "frames", "space", None, None),
            P("section", None, "frames", "space", None, None),
            P("section"),
            P("section", None, None, None),
            P("section", None, None, None),
            P("section", None, None),
        ),
        out_specs=P("section", None, "frames", "space", None, None),
        check_vma=False,
    )
```

```python
import jax
import jax.numpy as jnp
from jax import lax
import functools
from jax.experimental import pallas as pl
from jax.experimental.pallas import tpu as pltpu
from jax.sharding import PartitionSpec as P

HALO = 4


def section_kernel(
    m, n, cols, inner, num_frames, num_rows, total_frames, total_rows, k,
    offs_ref, prior_ref, noise_ref, w_hbm, out_ref, crop_ref, w_ref, sem, xl, xc, xr, nz,
):
    weight_copy = pltpu.make_async_copy(w_hbm.at[k], w_ref, sem)
    weight_copy.start()
    channels = w_ref.shape[-1]
    rows_in = m * n * cols
    rows_out = (m - 2) * (n - 2) * cols
    width = (m - num_frames) // 2
    prior = prior_ref[...].astype(jnp.float32)
    noise = noise_ref[...].astype(jnp.float32)
    weight_copy.wait()
    level = w_ref[13][0:1, :].astype(jnp.float32)
    noisy = prior + level * noise
    mean_sq = jnp.mean(noisy * noisy, axis=-1, keepdims=True)
    normalized = (noisy * lax.rsqrt(mean_sq + 1e-05)).astype(jnp.bfloat16).astype(jnp.float32)
    shape4 = (m, n, cols, channels)
    frame_at = offs_ref[0] - width + lax.broadcasted_iota(jnp.int32, shape4, 0)
    row_at = offs_ref[1] - width + lax.broadcasted_iota(jnp.int32, shape4, 1)
    inside = (frame_at >= 0) & (frame_at < total_frames) & (row_at >= 0) & (row_at < total_rows)
    inside = inside.reshape(m, n * cols, channels)
    normalized = jnp.where(inside, normalized.reshape(m, n * cols, channels), 0.0)
    normalized = normalized.reshape(rows_in, channels)
    col = lax.broadcasted_iota(jnp.int32, (rows_in, channels), 0) % cols
    left = jnp.where(col == 0, 0.0, pltpu.roll(normalized, 1, 0))
    right = jnp.where(col == cols - 1, 0.0, pltpu.roll(normalized, rows_in - 1, 0))
    xl[...] = left.reshape(m, n * cols, channels)
    xc[...] = normalized.reshape(m, n * cols, channels)
    xr[...] = right.reshape(m, n * cols, channels)
    nz[...] = noisy.reshape(m, n * cols, channels)
    views = (xl, xc, xr)
    acc = jnp.zeros((rows_out, channels), jnp.float32)
    for tap in range(9):
        a, b = tap // 3, tap % 3
        v = views[b][pl.ds(1, m - 2), pl.ds(a * cols, (n - 2) * cols), :]
        v = v.reshape(rows_out, channels).astype(jnp.bfloat16)
        acc = acc + jnp.dot(v, w_ref[tap], preferred_element_type=jnp.float32)
    for t in range(3):
        v = xc[pl.ds(t, m - 2), pl.ds(cols, (n - 2) * cols), :]
        v = v.reshape(rows_out, channels).astype(jnp.bfloat16)
        acc = acc + jnp.dot(v, w_ref[9 + t], preferred_element_type=jnp.float32)
    act = (acc / (1.0 + jnp.exp(-acc))).astype(jnp.bfloat16)
    est = jnp.dot(act, w_ref[12], preferred_element_type=jnp.float32)
    center = nz[pl.ds(1, m - 2), pl.ds(cols, (n - 2) * cols), :].reshape(rows_out, channels)
    result = center - level * est
    out_ref[...] = result.astype(out_ref.dtype)
    nz[pl.ds(0, m - 2), pl.ds(0, (n - 2) * cols), :] = result.reshape(m - 2, (n - 2) * cols, channels)
    crop = nz[pl.ds(inner, num_frames), pl.ds(inner * cols, num_rows * cols), :]
    crop_ref[...] = crop.reshape(num_frames * num_rows * cols, channels).astype(crop_ref.dtype)


def section_call(offs, prior, noise, packed, k, m, n, cols, num_frames, num_rows, totals):
    channels = packed.shape[-1]
    rows_in = m * n * cols
    rows_out = (m - 2) * (n - 2) * cols
    rows_crop = num_frames * num_rows * cols
    inner = (m - 2 - num_frames) // 2
    flops = 2 * rows_out * channels * channels * 13
    nbytes = 2 * 2 * rows_in * channels + 2 * 13 * channels * channels
    nbytes += 2 * (rows_out + rows_crop) * channels
    scratch = pltpu.VMEM((m, n * cols, channels), jnp.float32)
    smem = pl.BlockSpec(memory_space=pltpu.SMEM)
    vmem = pl.BlockSpec(memory_space=pltpu.VMEM)
    return pl.pallas_call(
        functools.partial(
            section_kernel, m, n, cols, inner, num_frames, num_rows, totals[0], totals[1], k
        ),
        out_shape=(
            jax.ShapeDtypeStruct((rows_out, channels), jnp.bfloat16),
            jax.ShapeDtypeStruct((rows_crop, channels), jnp.bfloat16),
        ),
        in_specs=[smem, vmem, vmem, pl.BlockSpec(memory_space=pl.ANY)],
        out_specs=(vmem, vmem),
        scratch_shapes=[
            pltpu.VMEM(packed.shape[1:], packed.dtype),
            pltpu.SemaphoreType.DMA(()),
        ]
        + [scratch] * 4,
        cost_estimate=pl.CostEstimate(
            flops=flops, bytes_accessed=nbytes, transcendentals=rows_out * channels
        ),
    )(offs, prior, noise, packed)


def extend(block, width, frame_dim, row_dim):
    for axis, dim in (("frames", frame_dim), ("space", row_dim)):
        count = lax.axis_size(axis)
        forward = [(i, i + 1) for i in range(count - 1)]
        backward = [(i + 1, i) for i in range(count - 1)]
        size = block.shape[dim]
        low = lax.ppermute(lax.slice_in_dim(block, size - width, size, axis=dim), axis, forward)
        high = lax.ppermute(lax.slice_in_dim(block, 0, width, axis=dim), axis, backward)
        block = jnp.concatenate([low, block, high], axis=dim)
    return block


def denoise(offs, previous, noise_part, packed, k, num_frames, num_rows, totals):
    num_videos, m, n, num_cols, channels = previous.shape
    outs = []
    crops = []
    for v in range(num_videos):
        out, crop = section_call(
            offs,
            previous[v].reshape(-1, channels),
            noise_part[v].reshape(-1, channels),
            packed,
            k,
            m,
            n,
            num_cols,
            num_frames,
            num_rows,
            totals,
        )
        outs.append(out.reshape(m - 2, n - 2, num_cols, channels))
        crops.append(crop)
    return jnp.stack(outs), jnp.stack(crops)


def on_device(
    base_frames, section_noise, noise_levels, spatial_kernel, temporal_kernel, output_weight
):
    place = lax.axis_index("section")
    sections = lax.axis_size("section")
    video_count, num_frames, num_rows = base_frames.shape[:3]
    per_device = video_count // sections
    halo = HALO
    noise_t = lax.all_to_all(section_noise[0], "section", 0, 0, tiled=True)
    noise_t = noise_t.reshape((sections, per_device) + noise_t.shape[1:])
    channels = spatial_kernel.shape[-1]
    noise_t, spatial_kernel, temporal_kernel, output_weight, noise_levels = lax.optimization_barrier(
        (noise_t, spatial_kernel, temporal_kernel, output_weight, noise_levels)
    )
    level_slab = jnp.broadcast_to(
        noise_levels.reshape(1, 1, 1, 1), (1, 1, channels, channels)
    ).astype(spatial_kernel.dtype)
    packed = jnp.concatenate(
        [spatial_kernel, temporal_kernel, output_weight[:, None], level_slab], axis=1
    )
    packed = lax.all_gather(packed, "section", tiled=True)
    incoming = lax.dynamic_slice_in_dim(base_frames, place * per_device, per_device, 0)
    offs = jnp.stack(
        [lax.axis_index("frames") * num_frames, lax.axis_index("space") * num_rows]
    ).astype(jnp.int32)
    totals = (num_frames * lax.axis_size("frames"), num_rows * lax.axis_size("space"))
    both = extend(jnp.concatenate([incoming[None], noise_t[:halo]], axis=0), halo, 2, 3)
    prior_ext = both[0]
    noise_round = both[1:]
    results = []
    for k in range(sections):
        j = k % halo
        if j == 0 and k > 0:
            prior_ext = extend(prior_ext, halo, 1, 2)
            noise_round = noise_next
        width = halo - j
        cut = halo - width
        noise_here = noise_round[
            j, :, cut : cut + num_frames + 2 * width, cut : cut + num_rows + 2 * width
        ]
        prior_ext, crop = denoise(
            offs, prior_ext, noise_here, packed, k, num_frames, num_rows, totals
        )
        results.append(crop)
        if j == 0 and k + halo < sections:
            later, _ = lax.optimization_barrier((noise_t[k + halo : k + 2 * halo], crop))
            noise_next = extend(later, halo, 2, 3)
    num_cols, channels = base_frames.shape[3:]
    stacked = jnp.stack(results).reshape(
        (sections, per_device, num_frames, num_rows, num_cols, channels)
    )
    return lax.all_to_all(stacked, "section", 0, 1, tiled=True)


def solution(mesh):
    return jax.shard_map(
        on_device,
        mesh=mesh,
        in_specs=(
            P(None, "frames", "space", None, None),
            P("section", None, "frames", "space", None, None),
            P("section"),
            P("section", None, None, None),
            P("section", None, None, None),
            P("section", None, None),
        ),
        out_specs=P("section", None, "frames", "space", None, None),
        check_vma=False,
    )
```

```python
import jax
import jax.numpy as jnp
from jax import lax
import functools
from jax.experimental import pallas as pl
from jax.experimental.pallas import tpu as pltpu
from jax.sharding import PartitionSpec as P

HALO = 4


def section_kernel(
    m, n, cols, inner, num_frames, num_rows, total_frames, total_rows, k,
    offs_ref, lv_ref, prior_ref, noise_ref, w_hbm, out_ref, crop_ref, w_ref, sem, xl, xc, xr, nz,
):
    weight_copy = pltpu.make_async_copy(w_hbm.at[k], w_ref, sem)
    weight_copy.start()
    channels = w_ref.shape[-1]
    rows_in = m * n * cols
    rows_out = (m - 2) * (n - 2) * cols
    width = (m - num_frames) // 2
    level = lv_ref[k]
    noisy = prior_ref[...].astype(jnp.float32) + level * noise_ref[...].astype(jnp.float32)
    mean_sq = jnp.mean(noisy * noisy, axis=-1, keepdims=True)
    normalized = (noisy * lax.rsqrt(mean_sq + 1e-05)).astype(jnp.bfloat16).astype(jnp.float32)
    shape4 = (m, n, cols, channels)
    frame_at = offs_ref[0] - width + lax.broadcasted_iota(jnp.int32, shape4, 0)
    row_at = offs_ref[1] - width + lax.broadcasted_iota(jnp.int32, shape4, 1)
    inside = (frame_at >= 0) & (frame_at < total_frames) & (row_at >= 0) & (row_at < total_rows)
    inside = inside.reshape(m, n * cols, channels)
    normalized = jnp.where(inside, normalized.reshape(m, n * cols, channels), 0.0)
    normalized = normalized.reshape(rows_in, channels)
    col = lax.broadcasted_iota(jnp.int32, (rows_in, channels), 0) % cols
    left = jnp.where(col == 0, 0.0, pltpu.roll(normalized, 1, 0))
    right = jnp.where(col == cols - 1, 0.0, pltpu.roll(normalized, rows_in - 1, 0))
    xl[...] = left.reshape(m, n * cols, channels)
    xc[...] = normalized.reshape(m, n * cols, channels)
    xr[...] = right.reshape(m, n * cols, channels)
    nz[...] = noisy.reshape(m, n * cols, channels)
    weight_copy.wait()
    views = (xl, xc, xr)
    acc = jnp.zeros((rows_out, channels), jnp.float32)
    for tap in range(9):
        a, b = tap // 3, tap % 3
        v = views[b][pl.ds(1, m - 2), pl.ds(a * cols, (n - 2) * cols), :]
        v = v.reshape(rows_out, channels).astype(jnp.bfloat16)
        acc = acc + jnp.dot(v, w_ref[tap], preferred_element_type=jnp.float32)
    for t in range(3):
        v = xc[pl.ds(t, m - 2), pl.ds(cols, (n - 2) * cols), :]
        v = v.reshape(rows_out, channels).astype(jnp.bfloat16)
        acc = acc + jnp.dot(v, w_ref[9 + t], preferred_element_type=jnp.float32)
    act = (acc / (1.0 + jnp.exp(-acc))).astype(jnp.bfloat16)
    est = jnp.dot(act, w_ref[12], preferred_element_type=jnp.float32)
    center = nz[pl.ds(1, m - 2), pl.ds(cols, (n - 2) * cols), :].reshape(rows_out, channels)
    result = center - level * est
    out_ref[...] = result.astype(out_ref.dtype)
    nz[pl.ds(0, m - 2), pl.ds(0, (n - 2) * cols), :] = result.reshape(m - 2, (n - 2) * cols, channels)
    crop = nz[pl.ds(inner, num_frames), pl.ds(inner * cols, num_rows * cols), :]
    crop_ref[...] = crop.reshape(num_frames * num_rows * cols, channels).astype(crop_ref.dtype)


def section_call(offs, levels, prior, noise, packed, k, m, n, cols, num_frames, num_rows, totals):
    channels = packed.shape[-1]
    rows_in = m * n * cols
    rows_out = (m - 2) * (n - 2) * cols
    rows_crop = num_frames * num_rows * cols
    inner = (m - 2 - num_frames) // 2
    flops = 2 * rows_out * channels * channels * 13
    nbytes = 2 * 2 * rows_in * channels + 2 * 13 * channels * channels
    nbytes += 2 * (rows_out + rows_crop) * channels
    scratch = pltpu.VMEM((m, n * cols, channels), jnp.float32)
    smem = pl.BlockSpec(memory_space=pltpu.SMEM)
    vmem = pl.BlockSpec(memory_space=pltpu.VMEM)
    return pl.pallas_call(
        functools.partial(
            section_kernel, m, n, cols, inner, num_frames, num_rows, totals[0], totals[1], k
        ),
        out_shape=(
            jax.ShapeDtypeStruct((rows_out, channels), jnp.bfloat16),
            jax.ShapeDtypeStruct((rows_crop, channels), jnp.bfloat16),
        ),
        in_specs=[smem, smem, vmem, vmem, pl.BlockSpec(memory_space=pl.ANY)],
        out_specs=(vmem, vmem),
        scratch_shapes=[
            pltpu.VMEM(packed.shape[1:], packed.dtype),
            pltpu.SemaphoreType.DMA(()),
        ]
        + [scratch] * 4,
        cost_estimate=pl.CostEstimate(
            flops=flops, bytes_accessed=nbytes, transcendentals=rows_out * channels
        ),
    )(offs, levels, prior, noise, packed)


def extend(block, width, frame_dim, row_dim):
    for axis, dim in (("frames", frame_dim), ("space", row_dim)):
        count = lax.axis_size(axis)
        forward = [(i, i + 1) for i in range(count - 1)]
        backward = [(i + 1, i) for i in range(count - 1)]
        size = block.shape[dim]
        low = lax.ppermute(lax.slice_in_dim(block, size - width, size, axis=dim), axis, forward)
        high = lax.ppermute(lax.slice_in_dim(block, 0, width, axis=dim), axis, backward)
        block = jnp.concatenate([low, block, high], axis=dim)
    return block


def denoise(offs, levels, previous, noise_part, packed, k, num_frames, num_rows, totals):
    num_videos, m, n, num_cols, channels = previous.shape
    outs = []
    crops = []
    for v in range(num_videos):
        out, crop = section_call(
            offs,
            levels,
            previous[v].reshape(-1, channels),
            noise_part[v].reshape(-1, channels),
            packed,
            k,
            m,
            n,
            num_cols,
            num_frames,
            num_rows,
            totals,
        )
        outs.append(out.reshape(m - 2, n - 2, num_cols, channels))
        crops.append(crop)
    return jnp.stack(outs), jnp.stack(crops)


def on_device(
    base_frames, section_noise, noise_levels, spatial_kernel, temporal_kernel, output_weight
):
    place = lax.axis_index("section")
    sections = lax.axis_size("section")
    video_count, num_frames, num_rows = base_frames.shape[:3]
    per_device = video_count // sections
    halo = HALO
    noise_t = lax.all_to_all(section_noise[0], "section", 0, 0, tiled=True)
    noise_t = noise_t.reshape((sections, per_device) + noise_t.shape[1:])
    channels = spatial_kernel.shape[-1]
    noise_t, spatial_kernel, temporal_kernel, output_weight, noise_levels = lax.optimization_barrier(
        (noise_t, spatial_kernel, temporal_kernel, output_weight, noise_levels)
    )
    level_slab = jnp.broadcast_to(
        noise_levels.reshape(1, 1, 1, 1), (1, 1, channels, channels)
    ).astype(spatial_kernel.dtype)
    packed = jnp.concatenate(
        [spatial_kernel, temporal_kernel, output_weight[:, None], level_slab], axis=1
    )
    packed = lax.all_gather(packed, "section", tiled=True)
    incoming = lax.dynamic_slice_in_dim(base_frames, place * per_device, per_device, 0)
    levels = packed[:, 13, 0, 0].astype(jnp.float32)
    offs = jnp.stack(
        [lax.axis_index("frames") * num_frames, lax.axis_index("space") * num_rows]
    ).astype(jnp.int32)
    totals = (num_frames * lax.axis_size("frames"), num_rows * lax.axis_size("space"))
    both = extend(jnp.concatenate([incoming[None], noise_t[:halo]], axis=0), halo, 2, 3)
    later_noise, both = lax.optimization_barrier((noise_t[halo:], both))
    prior_ext = both[0]
    noise_round = both[1:]
    results = []
    for k in range(sections):
        j = k % halo
        if j == 0 and k > 0:
            prior_ext = extend(prior_ext, halo, 1, 2)
            noise_round = noise_next
        width = halo - j
        cut = halo - width
        noise_here = noise_round[
            j, :, cut : cut + num_frames + 2 * width, cut : cut + num_rows + 2 * width
        ]
        prior_ext, crop = denoise(
            offs, levels, prior_ext, noise_here, packed, k, num_frames, num_rows, totals
        )
        results.append(crop)
        if j == 0 and k + halo < sections:
            later = later_noise[k : k + halo]
            noise_next = extend(later, halo, 2, 3)
    num_cols, channels = base_frames.shape[3:]
    stacked = jnp.stack(results).reshape(
        (sections, per_device, num_frames, num_rows, num_cols, channels)
    )
    return lax.all_to_all(stacked, "section", 0, 1, tiled=True)


def solution(mesh):
    return jax.shard_map(
        on_device,
        mesh=mesh,
        in_specs=(
            P(None, "frames", "space", None, None),
            P("section", None, "frames", "space", None, None),
            P("section"),
            P("section", None, None, None),
            P("section", None, None, None),
            P("section", None, None),
        ),
        out_specs=P("section", None, "frames", "space", None, None),
        check_vma=False,
    )
```
